32 devices in a mesh: dp: 4 (over z), expert: 4 (over y, x), tensor: 2 (over core).
Axes of the slice: x: 2, y: 2, z: 4, core: 2. Of those that a mesh axis runs over, the one named last changes fastest.
Arguments:
- tokens: bfloat16 [2048, 2048], P(('dp', 'expert')), may hold values from -6 to 6
- grad_out: bfloat16 [2048, 2048], P(('dp', 'expert')), may hold values from -6 to 6
- route_ids: int32 [2048, 8], P(('dp', 'expert')), may hold values from 0 to 15, all different within a row; in each aligned block of 128 rows (0 to 127, 128 to 255, ...) at most 72 rows name the same one
- gate_values: bfloat16 [2048, 8], P(('dp', 'expert')), may hold values from 0.049804688 to 0.5
- gate_proj: bfloat16 [16, 2048, 768], P(('dp', 'expert'), None, 'tensor'), may hold values from -0.125 to 0.125
- up_proj: bfloat16 [16, 2048, 768], P(('dp', 'expert'), None, 'tensor'), may hold values from -0.125 to 0.125
- down_proj: bfloat16 [16, 768, 2048], P(('dp', 'expert'), 'tensor'), may hold values from -0.21875 to 0.21875
Outputs:
- token_grad: bfloat16 [2048, 2048], P(('dp', 'expert'), 'tensor')
- gate_grad: bfloat16 [2048, 8], P(('dp', 'expert'))
- gate_proj_grad: bfloat16 [16, 2048, 768], P(('dp', 'expert'), None, 'tensor')
- up_proj_grad: bfloat16 [16, 2048, 768], P(('dp', 'expert'), None, 'tensor')
- down_proj_grad: bfloat16 [16, 768, 2048], P(('dp', 'expert'), 'tensor')
The draws below stay inside these ranges and needn't reach their ends.
Inputs may be any that keep to these rules, and one draw needn't show every extreme that they name: `route_ids`: each token names 8 different experts. Among the rows of one device (128 tokens), no expert is named more than 72 times, a bound that some block reaches.
All inputs are finite; a program needn't handle non-finite values.
Results may differ from the reference program's by a relative error of at most 0.008.
Values may be sent and summed in bfloat16 or wider, within the bound.
No kernel may reach another device: no remote copies, remote signals or barrier semaphores. Data moves between devices by JAX's collectives and lax.ppermute only.
A program may use at most 128 MiB of HBM per device.

```python
import math
import jax
import jax.numpy as jnp
import numpy as np
from jax import lax

D = 2048
FF = 768
TOP = 8
TOK_DEV = 128
EXPERTS = 16
MOST = 72
SLOTS = 1152
TOKENS = 2048
N_DP = 4
N_EXPERT = 4


def block_levels(key, dims, split, smallest, top_value):
    factor_of = 1.0
    for dim, shards_of in split:
        steps = jax.random.uniform(jax.random.fold_in(jax.random.fold_in(key, 6), dim), (shards_of,), jnp.float32, smallest / len(split), top_value / len(split))
        factor_of = factor_of * jnp.repeat(jnp.exp(steps), dims[dim] // shards_of).reshape((-1,) + (1,) * (len(dims) - 1 - dim))
    return factor_of


def shared_out(key, own, number, rows, amount, top, most, lean):
    sequence = jax.random.permutation(key, amount)
    crowded, usual = shares(amount, rows * top, most, lean, True), shares(amount, rows * top, most, lean, False)
    places = jnp.arange(amount)

    def named(lengths, turn):
        used = int((lengths > 0).sum())
        fixed = max(1, used // 4)
        passed = fixed + (places - fixed + turn * (used - fixed)) % max(1, amount - fixed)
        return jnp.zeros((amount,), jnp.int32).at[sequence[jnp.where(places < fixed, places, passed)]].set(jnp.asarray(lengths, jnp.int32))

    lengths = jnp.where(number % 4 == 0, named(crowded, number // 4), named(usual, number - number // 4 - 1))
    mixed = jax.random.permutation(jax.random.fold_in(own, 3), amount)
    source_of, sink = mixed[0:amount // 2 * 2:2], mixed[1:amount // 2 * 2:2]
    margin = jnp.minimum(lengths[source_of] - 1, most - lengths[sink]) // 2
    margin = jnp.where((source_of == sequence[0]) | (sink == sequence[0]) | (lengths[sink] == 0), 0, jnp.maximum(margin, 0))
    passed = jax.random.randint(jax.random.fold_in(own, 4), (amount // 2,), 0, 1 << 20) % (margin + 1)
    lengths = lengths.at[source_of].add(-passed).at[sink].add(passed)
    labels = jnp.searchsorted(jnp.cumsum(lengths), jnp.arange(rows * top), side="right").astype(jnp.int32)
    listing = labels.reshape(top, rows).T
    listing = listing[jax.random.permutation(jax.random.fold_in(own, 1), rows)]
    turn = jax.random.randint(jax.random.fold_in(own, 2), (rows, 1), 0, top)
    return jnp.take_along_axis(listing, (jnp.arange(top)[None, :] + turn) % top, axis=1)


def shares(count, total, most, slope, full):
    weights = [(1 << 20) // math.isqrt(rank ** slope) + 1 for rank in range(1, count + 1)]
    largest = most if full else min(most, max(-(-total // count), total * weights[0] // sum(weights)))
    least = 1 if total - largest >= count - 1 else 0
    counts, rest = [largest] + [least] * (count - 1), total - largest - least * (count - 1)
    while rest > 0:
        free = [i for i in range(1, count) if counts[i] < largest] or [i for i in range(1, count) if counts[i] < most]
        mass, left = sum([weights[i] for i in free]), rest
        for i in free:
            extra = min(most - counts[i], max(1, left * weights[i] // mass), rest)
            counts[i] = counts[i] + extra
            rest = rest - extra
    return np.array(counts)


def centred(own_key, dims, width, reach, split=(), kind=jnp.bfloat16):
    gain = block_levels(own_key, dims, split, -0.22, 0.18) if split else 1.0
    values = jax.random.normal(own_key, dims, jnp.float32) * width * gain
    return jnp.minimum(jnp.maximum(values, -reach), reach).astype(kind)


def setup_inputs(seed: int = 0) -> dict:
    key_of = jax.random.split(jax.random.key(seed), 8)
    tokens = centred(key_of[0], (TOKENS, D), 1.0, 6.0, ((0, 16),))
    grad_out = centred(key_of[1], (TOKENS, D), 1.0, 6.0, ((0, 16),))
    route_ids_keys = jax.random.split(jax.random.fold_in(key_of[2], 1), TOKENS // TOK_DEV)
    route_ids_turns = jax.random.permutation(jax.random.fold_in(key_of[2], 3), TOKENS // TOK_DEV)
    route_ids = jax.vmap(lambda own, number: shared_out(jax.random.fold_in(key_of[2], 2), own, number, TOK_DEV, EXPERTS, TOP, MOST, 2))(route_ids_keys, route_ids_turns).reshape((TOKENS, TOP))
    gate_values = jnp.clip(jnp.exp(math.log(0.5) - 2.306499 * jax.random.uniform(key_of[3], (TOKENS, TOP), jnp.float32) ** block_levels(key_of[3], (TOKENS, TOP), ((0, 16),), -0.2, 0.2)), 0.049804688, 0.5).astype(jnp.bfloat16)
    gate_proj = centred(key_of[4], (EXPERTS, D, FF), D ** -0.5, 0.125, ((0, 16), (2, 2)))
    up_proj = centred(key_of[5], (EXPERTS, D, FF), D ** -0.5, 0.125, ((0, 16), (2, 2)))
    down_proj = centred(key_of[6], (EXPERTS, FF, D), FF ** -0.5, 0.21875, ((0, 16), (1, 2)))
    return {"tokens": tokens, "grad_out": grad_out, "route_ids": route_ids, "gate_values": gate_values, "gate_proj": gate_proj, "up_proj": up_proj, "down_proj": down_proj}


def silu_parts(gate_pre):
    sig_gate = jax.nn.sigmoid(gate_pre)
    return sig_gate, gate_pre * sig_gate


def reference(tokens, grad_out, route_ids, gate_values, gate_proj, up_proj, down_proj):
    block_count = N_DP * N_EXPERT
    flat_ids = route_ids.reshape(block_count, TOK_DEV * TOP)
    expert_iota = jnp.arange(EXPERTS, dtype=jnp.int32)

    def block_positions(block_ids):
        one_hot = (block_ids[:, None] == expert_iota[None, :]).astype(jnp.int32)
        running = jnp.cumsum(one_hot, axis=0) - 1
        return jnp.sum(running * one_hot, axis=1).astype(jnp.int32)

    position = lax.map(block_positions, flat_ids)
    source_block = jnp.arange(block_count, dtype=jnp.int32)[:, None]
    global_slot = (flat_ids * SLOTS + source_block * MOST + position).reshape(-1).astype(jnp.int32)
    entry_of = jnp.full((EXPERTS * SLOTS,), -1, jnp.int32)
    entry_of = entry_of.at[global_slot].set(jnp.arange(TOKENS * TOP, dtype=jnp.int32))
    entry_of = entry_of.reshape(EXPERTS, SLOTS)
    gate_flat = gate_values.reshape(-1)

    def expert_step(carry, inputs):
        token_sum, gate_sum = carry
        entries, weight_g, weight_u, weight_d = inputs
        valid_mask = entries >= 0
        safe_entry = jnp.where(valid_mask, entries, 0).astype(jnp.int32)
        token_index = (safe_entry // TOP).astype(jnp.int32)
        routed_x = jnp.where(valid_mask[:, None], tokens[token_index], 0).astype(tokens.dtype)
        routed_dy = jnp.where(valid_mask[:, None], grad_out[token_index], 0).astype(grad_out.dtype)
        routed_gate = jnp.where(valid_mask, gate_flat[safe_entry], 0).astype(gate_values.dtype)
        gate_pre = jnp.dot(routed_x, weight_g, preferred_element_type=jnp.float32)
        up_pre = jnp.dot(routed_x, weight_u, preferred_element_type=jnp.float32)
        sig_gate, silu_gate = silu_parts(gate_pre)
        activation = (silu_gate * up_pre).astype(jnp.bfloat16)
        hidden_grad = jnp.dot(routed_dy, weight_d.T, preferred_element_type=jnp.float32)
        slot_gate = jnp.sum(hidden_grad * activation.astype(jnp.float32), axis=1).astype(jnp.bfloat16)
        row_gate = routed_gate.astype(jnp.float32)[:, None]
        scaled = row_gate * hidden_grad
        up_grad = (scaled * silu_gate).astype(jnp.bfloat16)
        pre_grad = (scaled * up_pre * sig_gate * (1.0 + gate_pre * (1.0 - sig_gate))).astype(jnp.bfloat16)
        grad_g = jnp.dot(routed_x.T, pre_grad, preferred_element_type=jnp.float32).astype(jnp.bfloat16)
        grad_u = jnp.dot(routed_x.T, up_grad, preferred_element_type=jnp.float32).astype(jnp.bfloat16)
        weighted = (row_gate * activation.astype(jnp.float32)).astype(jnp.bfloat16)
        grad_d = jnp.dot(weighted.T, routed_dy, preferred_element_type=jnp.float32).astype(jnp.bfloat16)
        routed_grad = (jnp.dot(pre_grad, weight_g.T, preferred_element_type=jnp.float32)
                       + jnp.dot(up_grad, weight_u.T, preferred_element_type=jnp.float32)).astype(jnp.bfloat16)
        target_row = jnp.where(valid_mask, token_index, TOKENS).astype(jnp.int32)
        token_sum = token_sum.at[target_row].add(routed_grad.astype(jnp.float32), mode="drop")
        target_entry = jnp.where(valid_mask, safe_entry, TOKENS * TOP).astype(jnp.int32)
        gate_sum = gate_sum.at[target_entry].set(slot_gate.astype(jnp.float32), mode="drop")
        return (token_sum, gate_sum), (grad_g, grad_u, grad_d)

    start = (jnp.zeros((TOKENS, D), jnp.float32), jnp.zeros((TOKENS * TOP,), jnp.float32))
    (token_sum, gate_sum), (grad_g, grad_u, grad_d) = lax.scan(
        expert_step, start, (entry_of, gate_proj, up_proj, down_proj))
    token_grad = token_sum.astype(jnp.bfloat16)
    gate_grad = gate_sum.reshape(TOKENS, TOP).astype(jnp.bfloat16)
    return (token_grad, gate_grad, grad_g, grad_u, grad_d)
```

```python
import jax
import jax.numpy as jnp
from jax import lax
from jax.sharding import PartitionSpec as P


def on_device(tokens, grad_out, route_ids, gate_values, gate_proj, up_proj, down_proj):
    tok_rows, features = tokens.shape
    top_count = route_ids.shape[1]
    n_dp = lax.axis_size("dp")
    n_ex = lax.axis_size("expert")
    groups = n_dp * n_ex
    capacity = max(2, tok_rows * top_count * 9 // (8 * groups))
    plane = lax.axis_index("dp")
    core = lax.axis_index("tensor")
    col_rows = n_dp * tok_rows
    plane_slots = n_dp * capacity
    slots = n_ex * plane_slots

    ids_all = lax.all_gather(route_ids, "dp", tiled=True)
    gates_all = lax.all_gather(gate_values, "dp", tiled=True)

    carried = jnp.where(core == 0, tokens, grad_out)
    carried_all = lax.all_gather(carried, "dp", tiled=True)

    routes = tok_rows * top_count
    ids_blk = ids_all.reshape(n_dp, routes)
    local_ex = ids_blk - plane * n_ex
    in_plane = (local_ex >= 0) & (local_ex < n_ex)
    one_hot = (local_ex[:, :, None] == jnp.arange(n_ex, dtype=jnp.int32)[None, None, :])
    one_hot_b = one_hot.astype(jnp.bfloat16)
    r_iota = jnp.arange(routes, dtype=jnp.int32)
    earlier = (r_iota[None, :] < r_iota[:, None]).astype(jnp.bfloat16)
    running = jnp.einsum(
        "ab,nbe->nae", earlier, one_hot_b, preferred_element_type=jnp.float32
    )
    position = jnp.sum(running * one_hot.astype(jnp.float32), axis=2).astype(jnp.int32)
    blk = jnp.arange(n_dp, dtype=jnp.int32)[:, None]
    slot_of = jnp.where(in_plane, local_ex * plane_slots + blk * capacity + position, -1)
    slot_of = slot_of.reshape(col_rows, top_count)

    s_iota = jnp.arange(slots, dtype=jnp.int32)
    match = slot_of[None, :, :] == s_iota[:, None, None]
    select = jnp.sum(match.astype(jnp.bfloat16), axis=2)
    send = jnp.dot(select, carried_all, preferred_element_type=jnp.float32).astype(tokens.dtype)
    send_gate = jnp.sum(
        jnp.where(match, gates_all.astype(jnp.float32)[None, :, :], 0.0), axis=(1, 2)
    ).astype(gate_values.dtype)

    recv = lax.all_to_all(send, "expert", split_axis=0, concat_axis=0, tiled=True)
    routed_gate = lax.all_to_all(send_gate, "expert", split_axis=0, concat_axis=0, tiled=True)
    both = lax.all_gather(recv, "tensor")
    routed_x = both[0]
    routed_dy = both[1]

    weight_g = gate_proj[0]
    weight_u = up_proj[0]
    weight_d = down_proj[0]
    gate_pre = jnp.dot(routed_x, weight_g, preferred_element_type=jnp.float32)
    up_pre = jnp.dot(routed_x, weight_u, preferred_element_type=jnp.float32)
    sig_gate = jax.nn.sigmoid(gate_pre)
    silu_gate = gate_pre * sig_gate
    activation = (silu_gate * up_pre).astype(jnp.bfloat16)
    hidden_grad = lax.dot_general(
        routed_dy, weight_d, (((1,), (1,)), ((), ())), preferred_element_type=jnp.float32
    )
    gate_terms = jnp.sum(hidden_grad * activation.astype(jnp.float32), axis=1)
    row_gate = routed_gate.astype(jnp.float32)[:, None]
    scaled = row_gate * hidden_grad
    up_grad = (scaled * silu_gate).astype(jnp.bfloat16)
    pre_grad = (scaled * up_pre * sig_gate * (1.0 + gate_pre * (1.0 - sig_gate))).astype(
        jnp.bfloat16
    )
    grad_g = lax.dot_general(
        routed_x, pre_grad, (((0,), (0,)), ((), ())), preferred_element_type=jnp.float32
    ).astype(jnp.bfloat16)
    grad_u = lax.dot_general(
        routed_x, up_grad, (((0,), (0,)), ((), ())), preferred_element_type=jnp.float32
    ).astype(jnp.bfloat16)
    weighted = (row_gate * activation.astype(jnp.float32)).astype(jnp.bfloat16)
    grad_d = lax.dot_general(
        weighted, routed_dy, (((0,), (0,)), ((), ())), preferred_element_type=jnp.float32
    ).astype(jnp.bfloat16)
    partial_value = lax.dot_general(
        pre_grad, weight_g, (((1,), (1,)), ((), ())), preferred_element_type=jnp.float32
    ) + lax.dot_general(
        up_grad, weight_u, (((1,), (1,)), ((), ())), preferred_element_type=jnp.float32
    )
    routed_grad = lax.psum_scatter(partial_value, "tensor", scatter_dimension=1, tiled=True).astype(
        jnp.bfloat16
    )
    slot_gate = lax.psum(gate_terms, "tensor").astype(jnp.bfloat16)

    back_rows = lax.all_to_all(routed_grad, "expert", split_axis=0, concat_axis=0, tiled=True)
    back_gate = lax.all_to_all(slot_gate, "expert", split_axis=0, concat_axis=0, tiled=True)

    col_grad = lax.dot_general(
        select, back_rows, (((0,), (0,)), ((), ())), preferred_element_type=jnp.float32
    )
    token_grad = lax.psum_scatter(col_grad, "dp", scatter_dimension=0, tiled=True).astype(
        jnp.bfloat16
    )
    col_gate = jnp.sum(
        jnp.where(match, back_gate.astype(jnp.float32)[:, None, None], 0.0), axis=0
    )
    gate_grad = lax.psum_scatter(col_gate, "dp", scatter_dimension=0, tiled=True).astype(
        jnp.bfloat16
    )
    return (token_grad, gate_grad, grad_g[None], grad_u[None], grad_d[None])


def solution(mesh):
    in_specs = (
        P(("dp", "expert"), None),
        P(("dp", "expert"), None),
        P(("dp", "expert"), None),
        P(("dp", "expert"), None),
        P(("dp", "expert"), None, "tensor"),
        P(("dp", "expert"), None, "tensor"),
        P(("dp", "expert"), "tensor", None),
    )
    out_specs = (
        P(("dp", "expert"), "tensor"),
        P(("dp", "expert"), None),
        P(("dp", "expert"), None, "tensor"),
        P(("dp", "expert"), None, "tensor"),
        P(("dp", "expert"), "tensor", None),
    )
    return jax.shard_map(
        on_device, mesh=mesh, in_specs=in_specs, out_specs=out_specs, check_vma=False
    )
```

```python
import jax
import jax.numpy as jnp
from jax import lax
from jax.sharding import PartitionSpec as P


def on_device(tokens, grad_out, route_ids, gate_values, gate_proj, up_proj, down_proj):
    tok_rows, features = tokens.shape
    top_count = route_ids.shape[1]
    n_dp = lax.axis_size("dp")
    n_ex = lax.axis_size("expert")
    groups = n_dp * n_ex
    capacity = max(2, tok_rows * top_count * 9 // (8 * groups))
    plane = lax.axis_index("dp")
    core = lax.axis_index("tensor")
    col_rows = n_dp * tok_rows
    slots = n_ex * n_dp * capacity

    carried = jnp.where(core == 0, tokens, grad_out)
    aux = jnp.concatenate([route_ids.astype(tokens.dtype), gate_values.astype(tokens.dtype)], axis=1)
    pad = (-(features + aux.shape[1])) % 128
    aux = jnp.pad(aux, ((0, 0), (0, pad)))
    ext_all = lax.all_gather(jnp.concatenate([carried, aux], axis=1), "dp", tiled=True)
    carried_all = ext_all[:, :features].reshape(n_dp, tok_rows, features)
    ids_all = ext_all[:, features:features + top_count].astype(jnp.int32)
    gates_all = ext_all[:, features + top_count:features + 2 * top_count].astype(jnp.float32)

    routes = tok_rows * top_count
    ids_blk = ids_all.reshape(n_dp, routes)
    local_ex = ids_blk - plane * n_ex
    in_plane = (local_ex >= 0) & (local_ex < n_ex)
    one_hot = (local_ex[:, :, None] == jnp.arange(n_ex, dtype=jnp.int32)[None, None, :])
    one_hot_b = one_hot.astype(jnp.bfloat16)
    r_iota = jnp.arange(routes, dtype=jnp.int32)
    earlier = (r_iota[None, :] < r_iota[:, None]).astype(jnp.bfloat16)
    running = jnp.einsum(
        "ab,nbe->nae", earlier, one_hot_b, preferred_element_type=jnp.float32
    )
    position = jnp.sum(running * one_hot.astype(jnp.float32), axis=2).astype(jnp.int32)
    key = jnp.where(in_plane, local_ex * capacity + position, -1)
    key = key.reshape(n_dp, tok_rows, top_count)

    q_iota = jnp.arange(n_ex * capacity, dtype=jnp.int32)
    match = key[:, None, :, :] == q_iota[None, :, None, None]
    select = jnp.sum(match.astype(jnp.bfloat16), axis=3)
    gates_blk = gates_all.reshape(n_dp, tok_rows, top_count)
    send = jnp.einsum(
        "bqt,btf->bqf", select, carried_all, preferred_element_type=jnp.float32
    ).astype(tokens.dtype)
    send_gate = jnp.sum(jnp.where(match, gates_blk[:, None, :, :], 0.0), axis=(2, 3)).astype(
        gate_values.dtype
    )

    recv = lax.all_to_all(
        send.reshape(n_dp, n_ex, capacity, features), "expert", split_axis=1, concat_axis=1, tiled=True
    ).reshape(slots, features)
    routed_gate = lax.all_to_all(
        send_gate.reshape(n_dp, n_ex, capacity), "expert", split_axis=1, concat_axis=1, tiled=True
    ).reshape(slots)
    both = lax.all_gather(recv, "tensor")
    routed_x = both[0]
    routed_dy = both[1]

    weight_g = gate_proj[0]
    weight_u = up_proj[0]
    weight_d = down_proj[0]
    gate_pre = jnp.dot(routed_x, weight_g, preferred_element_type=jnp.float32)
    up_pre = jnp.dot(routed_x, weight_u, preferred_element_type=jnp.float32)
    sig_gate = jax.nn.sigmoid(gate_pre)
    silu_gate = gate_pre * sig_gate
    activation = (silu_gate * up_pre).astype(jnp.bfloat16)
    hidden_grad = lax.dot_general(
        routed_dy, weight_d, (((1,), (1,)), ((), ())), preferred_element_type=jnp.float32
    )
    gate_terms = jnp.sum(hidden_grad * activation.astype(jnp.float32), axis=1)
    row_gate = routed_gate.astype(jnp.float32)[:, None]
    scaled = row_gate * hidden_grad
    up_grad = (scaled * silu_gate).astype(jnp.bfloat16)
    pre_grad = (scaled * up_pre * sig_gate * (1.0 + gate_pre * (1.0 - sig_gate))).astype(
        jnp.bfloat16
    )
    grad_g = lax.dot_general(
        routed_x, pre_grad, (((0,), (0,)), ((), ())), preferred_element_type=jnp.float32
    ).astype(jnp.bfloat16)
    grad_u = lax.dot_general(
        routed_x, up_grad, (((0,), (0,)), ((), ())), preferred_element_type=jnp.float32
    ).astype(jnp.bfloat16)
    weighted = (row_gate * activation.astype(jnp.float32)).astype(jnp.bfloat16)
    grad_d = lax.dot_general(
        weighted, routed_dy, (((0,), (0,)), ((), ())), preferred_element_type=jnp.float32
    ).astype(jnp.bfloat16)
    partial_value = lax.dot_general(
        pre_grad, weight_g, (((1,), (1,)), ((), ())), preferred_element_type=jnp.float32
    ) + lax.dot_general(
        up_grad, weight_u, (((1,), (1,)), ((), ())), preferred_element_type=jnp.float32
    )
    routed_grad = lax.psum_scatter(partial_value, "tensor", scatter_dimension=1, tiled=True).astype(
        jnp.bfloat16
    )
    slot_gate = lax.psum(gate_terms, "tensor").astype(jnp.bfloat16)

    half = routed_grad.shape[1]
    back_rows = lax.all_to_all(
        routed_grad.reshape(n_dp, n_ex, capacity, half), "expert", split_axis=1, concat_axis=1, tiled=True
    ).reshape(n_dp, n_ex * capacity, half)
    back_gate = lax.all_to_all(
        slot_gate.reshape(n_dp, n_ex, capacity), "expert", split_axis=1, concat_axis=1, tiled=True
    ).reshape(n_dp, n_ex * capacity)

    col_grad = jnp.einsum(
        "bqt,bqf->btf", select, back_rows, preferred_element_type=jnp.float32
    ).reshape(col_rows, half)
    token_grad = lax.psum_scatter(col_grad, "dp", scatter_dimension=0, tiled=True).astype(
        jnp.bfloat16
    )
    col_gate = jnp.sum(
        jnp.where(match, back_gate.astype(jnp.float32)[:, :, None, None], 0.0), axis=1
    ).reshape(col_rows, top_count)
    gate_grad = lax.psum_scatter(col_gate, "dp", scatter_dimension=0, tiled=True).astype(
        jnp.bfloat16
    )
    return (token_grad, gate_grad, grad_g[None], grad_u[None], grad_d[None])


def solution(mesh):
    in_specs = (
        P(("dp", "expert"), None),
        P(("dp", "expert"), None),
        P(("dp", "expert"), None),
        P(("dp", "expert"), None),
        P(("dp", "expert"), None, "tensor"),
        P(("dp", "expert"), None, "tensor"),
        P(("dp", "expert"), "tensor", None),
    )
    out_specs = (
        P(("dp", "expert"), "tensor"),
        P(("dp", "expert"), None),
        P(("dp", "expert"), None, "tensor"),
        P(("dp", "expert"), None, "tensor"),
        P(("dp", "expert"), "tensor", None),
    )
    return jax.shard_map(
        on_device, mesh=mesh, in_specs=in_specs, out_specs=out_specs, check_vma=False
    )
```

```python
import jax
import jax.numpy as jnp
from jax import lax
from jax.sharding import PartitionSpec as P


def on_device(tokens, grad_out, route_ids, gate_values, gate_proj, up_proj, down_proj):
    tok_rows, features = tokens.shape
    top_count = route_ids.shape[1]
    n_dp = lax.axis_size("dp")
    n_ex = lax.axis_size("expert")
    groups = n_dp * n_ex
    capacity = max(2, tok_rows * top_count * 9 // (8 * groups))
    plane = lax.axis_index("dp")
    core = lax.axis_index("tensor")
    routes = tok_rows * top_count
    block_slots = n_ex * capacity
    lanes = 128

    carried = jnp.where(core == 0, tokens, grad_out)
    aux = jnp.concatenate([route_ids.astype(tokens.dtype), gate_values.astype(tokens.dtype)], axis=1)
    aux = jnp.pad(aux, ((0, 0), (0, lanes - aux.shape[1])))
    ext = jnp.concatenate([carried, aux], axis=1)
    blocks = [ext] + [
        lax.ppermute(ext, "dp", [(i, (i + s) % n_dp) for i in range(n_dp)])
        for s in range(1, n_dp)
    ]

    r_iota = jnp.arange(routes, dtype=jnp.int32)
    earlier = (r_iota[None, :] < r_iota[:, None]).astype(jnp.bfloat16)
    e_iota = jnp.arange(n_ex, dtype=jnp.int32)
    q_iota = jnp.arange(block_slots, dtype=jnp.int32)

    weight_g = gate_proj[0]
    weight_u = up_proj[0]
    weight_d = down_proj[0]
    acc_g = acc_u = acc_d = None
    col_parts = []
    for blk in blocks:
        carried_b = blk[:, :features]
        ids_b = blk[:, features:features + top_count].astype(jnp.int32)
        gates_b = blk[:, features + top_count:features + 2 * top_count].astype(jnp.float32)

        local_ex = ids_b.reshape(routes) - plane * n_ex
        in_plane = (local_ex >= 0) & (local_ex < n_ex)
        one_hot = local_ex[:, None] == e_iota[None, :]
        running = jnp.dot(earlier, one_hot.astype(jnp.bfloat16), preferred_element_type=jnp.float32)
        position = jnp.sum(running * one_hot.astype(jnp.float32), axis=1).astype(jnp.int32)
        key = jnp.where(in_plane, local_ex * capacity + position, -1).reshape(tok_rows, top_count)
        match = key[None, :, :] == q_iota[:, None, None]
        select = jnp.sum(match.astype(jnp.bfloat16), axis=2)
        send_rows = jnp.dot(select, carried_b, preferred_element_type=jnp.float32).astype(tokens.dtype)
        send_gate = jnp.sum(jnp.where(match, gates_b[None, :, :], 0.0), axis=(1, 2))
        gate_cols = jnp.pad(send_gate.astype(tokens.dtype)[:, None], ((0, 0), (0, lanes - 1)))
        send = jnp.concatenate([send_rows, gate_cols], axis=1)

        recv = lax.all_to_all(
            send.reshape(n_ex, capacity, features + lanes), "expert", split_axis=0, concat_axis=0, tiled=True
        ).reshape(block_slots, features + lanes)
        both = lax.all_gather(recv, "tensor")
        routed_x = both[0, :, :features]
        routed_dy = both[1, :, :features]
        routed_gate = both[0, :, features]

        gate_pre = jnp.dot(routed_x, weight_g, preferred_element_type=jnp.float32)
        up_pre = jnp.dot(routed_x, weight_u, preferred_element_type=jnp.float32)
        sig_gate = jax.nn.sigmoid(gate_pre)
        silu_gate = gate_pre * sig_gate
        activation = (silu_gate * up_pre).astype(jnp.bfloat16)
        hidden_grad = lax.dot_general(
            routed_dy, weight_d, (((1,), (1,)), ((), ())), preferred_element_type=jnp.float32
        )
        gate_terms = jnp.sum(hidden_grad * activation.astype(jnp.float32), axis=1)
        row_gate = routed_gate.astype(jnp.float32)[:, None]
        scaled = row_gate * hidden_grad
        up_grad = (scaled * silu_gate).astype(jnp.bfloat16)
        pre_grad = (scaled * up_pre * sig_gate * (1.0 + gate_pre * (1.0 - sig_gate))).astype(
            jnp.bfloat16
        )
        part_g = lax.dot_general(
            routed_x, pre_grad, (((0,), (0,)), ((), ())), preferred_element_type=jnp.float32
        )
        part_u = lax.dot_general(
            routed_x, up_grad, (((0,), (0,)), ((), ())), preferred_element_type=jnp.float32
        )
        weighted = (row_gate * activation.astype(jnp.float32)).astype(jnp.bfloat16)
        part_d = lax.dot_general(
            weighted, routed_dy, (((0,), (0,)), ((), ())), preferred_element_type=jnp.float32
        )
        if acc_g is None:
            acc_g, acc_u, acc_d = part_g, part_u, part_d
        else:
            acc_g, acc_u, acc_d = acc_g + part_g, acc_u + part_u, acc_d + part_d
        gate_col = jnp.pad(gate_terms[:, None], ((0, 0), (0, lanes - 1)))
        pieces = []
        half = features // 2
        for h in range(2):
            rows = slice(h * half, (h + 1) * half)
            pieces.append(
                lax.dot_general(
                    pre_grad, weight_g[rows], (((1,), (1,)), ((), ())), preferred_element_type=jnp.float32
                ) + lax.dot_general(
                    up_grad, weight_u[rows], (((1,), (1,)), ((), ())), preferred_element_type=jnp.float32
                )
            )
            pieces.append(gate_col)
        ret = lax.psum_scatter(
            jnp.concatenate(pieces, axis=1), "tensor", scatter_dimension=1, tiled=True
        ).astype(jnp.bfloat16)
        back = lax.all_to_all(
            ret.reshape(n_ex, capacity, half + lanes), "expert", split_axis=0, concat_axis=0, tiled=True
        ).reshape(block_slots, half + lanes)

        col_grad = lax.dot_general(
            select, back[:, :half], (((0,), (0,)), ((), ())), preferred_element_type=jnp.float32
        )
        col_gate = jnp.sum(
            jnp.where(match, back[:, half].astype(jnp.float32)[:, None, None], 0.0), axis=0
        )
        col_parts.append(
            jnp.concatenate(
                [col_grad, jnp.pad(col_gate, ((0, 0), (0, lanes - top_count)))], axis=1
            )
        )

    by_shift = jnp.stack(col_parts)
    order = (plane - jnp.arange(n_dp, dtype=jnp.int32)) % n_dp
    by_dest = jnp.take(by_shift, order, axis=0)
    width = by_dest.shape[2]
    total = lax.psum_scatter(
        by_dest.reshape(n_dp * tok_rows, width), "dp", scatter_dimension=0, tiled=True
    )
    half = total.shape[1] - lanes
    token_grad = total[:, :half].astype(jnp.bfloat16)
    gate_grad = total[:, half:half + top_count].astype(jnp.bfloat16)
    grad_g = acc_g.astype(jnp.bfloat16)
    grad_u = acc_u.astype(jnp.bfloat16)
    grad_d = acc_d.astype(jnp.bfloat16)
    return (token_grad, gate_grad, grad_g[None], grad_u[None], grad_d[None])


def solution(mesh):
    in_specs = (
        P(("dp", "expert"), None),
        P(("dp", "expert"), None),
        P(("dp", "expert"), None),
        P(("dp", "expert"), None),
        P(("dp", "expert"), None, "tensor"),
        P(("dp", "expert"), None, "tensor"),
        P(("dp", "expert"), "tensor", None),
    )
    out_specs = (
        P(("dp", "expert"), "tensor"),
        P(("dp", "expert"), None),
        P(("dp", "expert"), None, "tensor"),
        P(("dp", "expert"), None, "tensor"),
        P(("dp", "expert"), "tensor", None),
    )
    return jax.shard_map(
        on_device, mesh=mesh, in_specs=in_specs, out_specs=out_specs, check_vma=False
    )
```

```python
import jax
import jax.numpy as jnp
from jax import lax
from jax.sharding import PartitionSpec as P


def on_device(tokens, grad_out, route_ids, gate_values, gate_proj, up_proj, down_proj):
    tok_rows, features = tokens.shape
    top_count = route_ids.shape[1]
    n_dp = lax.axis_size("dp")
    n_ex = lax.axis_size("expert")
    groups = n_dp * n_ex
    capacity = max(2, tok_rows * top_count * 9 // (8 * groups))
    plane = lax.axis_index("dp")
    core = lax.axis_index("tensor")
    routes = tok_rows * top_count
    block_slots = n_ex * capacity
    lanes = 128

    carried = jnp.where(core == 0, tokens, grad_out)
    aux = jnp.concatenate([route_ids.astype(tokens.dtype), gate_values.astype(tokens.dtype)], axis=1)
    aux = jnp.pad(aux, ((0, 0), (0, lanes - aux.shape[1])))
    ext = jnp.concatenate([carried, aux], axis=1)
    blocks = [ext] + [
        lax.ppermute(ext, "dp", [(i, (i + s) % n_dp) for i in range(n_dp)])
        for s in range(1, n_dp)
    ]

    r_iota = jnp.arange(routes, dtype=jnp.int32)
    earlier = (r_iota[None, :] < r_iota[:, None]).astype(jnp.bfloat16)
    e_iota = jnp.arange(n_ex, dtype=jnp.int32)
    q_iota = jnp.arange(block_slots, dtype=jnp.int32)

    weight_g = gate_proj[0]
    weight_u = up_proj[0]
    weight_d = down_proj[0]
    acc_g = acc_u = acc_d = None
    col_parts = []
    for s, blk in enumerate(blocks):
        carried_b = blk[:, :features]
        ids_b = blk[:, features:features + top_count].astype(jnp.int32)
        gates_b = blk[:, features + top_count:features + 2 * top_count].astype(jnp.float32)

        local_ex = ids_b.reshape(routes) - plane * n_ex
        in_plane = (local_ex >= 0) & (local_ex < n_ex)
        one_hot = local_ex[:, None] == e_iota[None, :]
        running = jnp.dot(earlier, one_hot.astype(jnp.bfloat16), preferred_element_type=jnp.float32)
        position = jnp.sum(running * one_hot.astype(jnp.float32), axis=1).astype(jnp.int32)
        key = jnp.where(in_plane, local_ex * capacity + position, -1).reshape(tok_rows, top_count)
        match = key[None, :, :] == q_iota[:, None, None]
        select = jnp.sum(match.astype(jnp.bfloat16), axis=2)
        send_rows = jnp.dot(select, carried_b, preferred_element_type=jnp.float32).astype(tokens.dtype)
        send_gate = jnp.sum(jnp.where(match, gates_b[None, :, :], 0.0), axis=(1, 2))
        gate_cols = jnp.pad(send_gate.astype(tokens.dtype)[:, None], ((0, 0), (0, lanes - 1)))
        send = jnp.concatenate([send_rows, gate_cols], axis=1)

        recv = lax.all_to_all(
            send.reshape(n_ex, capacity, features + lanes), "expert", split_axis=0, concat_axis=0, tiled=True
        ).reshape(block_slots, features + lanes)
        both = lax.all_gather(recv, "tensor")
        routed_x = both[0, :, :features]
        routed_dy = both[1, :, :features]
        routed_gate = both[0, :, features]

        gate_pre = jnp.dot(routed_x, weight_g, preferred_element_type=jnp.float32)
        up_pre = jnp.dot(routed_x, weight_u, preferred_element_type=jnp.float32)
        sig_gate = jax.nn.sigmoid(gate_pre)
        silu_gate = gate_pre * sig_gate
        activation = (silu_gate * up_pre).astype(jnp.bfloat16)
        hidden_grad = lax.dot_general(
            routed_dy, weight_d, (((1,), (1,)), ((), ())), preferred_element_type=jnp.float32
        )
        gate_terms = jnp.sum(hidden_grad * activation.astype(jnp.float32), axis=1)
        row_gate = routed_gate.astype(jnp.float32)[:, None]
        scaled = row_gate * hidden_grad
        up_grad = (scaled * silu_gate).astype(jnp.bfloat16)
        pre_grad = (scaled * up_pre * sig_gate * (1.0 + gate_pre * (1.0 - sig_gate))).astype(
            jnp.bfloat16
        )
        part_g = lax.dot_general(
            routed_x, pre_grad, (((0,), (0,)), ((), ())), preferred_element_type=jnp.float32
        )
        part_u = lax.dot_general(
            routed_x, up_grad, (((0,), (0,)), ((), ())), preferred_element_type=jnp.float32
        )
        weighted = (row_gate * activation.astype(jnp.float32)).astype(jnp.bfloat16)
        part_d = lax.dot_general(
            weighted, routed_dy, (((0,), (0,)), ((), ())), preferred_element_type=jnp.float32
        )
        if acc_g is None:
            acc_g, acc_u, acc_d = part_g, part_u, part_d
        else:
            acc_g, acc_u, acc_d = acc_g + part_g, acc_u + part_u, acc_d + part_d
        gate_col = jnp.pad(gate_terms[:, None], ((0, 0), (0, lanes - 1)))
        pieces = []
        half = features // 2
        for h in range(2):
            rows = slice(h * half, (h + 1) * half)
            pieces.append(
                lax.dot_general(
                    pre_grad, weight_g[rows], (((1,), (1,)), ((), ())), preferred_element_type=jnp.float32
                ) + lax.dot_general(
                    up_grad, weight_u[rows], (((1,), (1,)), ((), ())), preferred_element_type=jnp.float32
                )
            )
            pieces.append(gate_col)
        ret = lax.psum_scatter(
            jnp.concatenate(pieces, axis=1), "tensor", scatter_dimension=1, tiled=True
        ).astype(jnp.bfloat16)
        back = lax.all_to_all(
            ret.reshape(n_ex, capacity, half + lanes), "expert", split_axis=0, concat_axis=0, tiled=True
        ).reshape(block_slots, half + lanes)

        col_grad = lax.dot_general(
            select, back[:, :half], (((0,), (0,)), ((), ())), preferred_element_type=jnp.float32
        )
        col_gate = jnp.sum(
            jnp.where(match, back[:, half].astype(jnp.float32)[:, None, None], 0.0), axis=0
        )
        part = jnp.concatenate(
            [col_grad, jnp.pad(col_gate, ((0, 0), (0, lanes - top_count)))], axis=1
        ).astype(jnp.bfloat16)
        if s:
            part = lax.ppermute(part, "dp", [(i, (i - s) % n_dp) for i in range(n_dp)])
        col_parts.append(part.astype(jnp.float32))

    total = sum(col_parts[1:], col_parts[0])
    half = total.shape[1] - lanes
    token_grad = total[:, :half].astype(jnp.bfloat16)
    gate_grad = total[:, half:half + top_count].astype(jnp.bfloat16)
    grad_g = acc_g.astype(jnp.bfloat16)
    grad_u = acc_u.astype(jnp.bfloat16)
    grad_d = acc_d.astype(jnp.bfloat16)
    return (token_grad, gate_grad, grad_g[None], grad_u[None], grad_d[None])


def solution(mesh):
    in_specs = (
        P(("dp", "expert"), None),
        P(("dp", "expert"), None),
        P(("dp", "expert"), None),
        P(("dp", "expert"), None),
        P(("dp", "expert"), None, "tensor"),
        P(("dp", "expert"), None, "tensor"),
        P(("dp", "expert"), "tensor", None),
    )
    out_specs = (
        P(("dp", "expert"), "tensor"),
        P(("dp", "expert"), None),
        P(("dp", "expert"), None, "tensor"),
        P(("dp", "expert"), None, "tensor"),
        P(("dp", "expert"), "tensor", None),
    )
    return jax.shard_map(
        on_device, mesh=mesh, in_specs=in_specs, out_specs=out_specs, check_vma=False
    )
```

```python
import jax
import jax.numpy as jnp
from jax import lax
from jax.sharding import PartitionSpec as P


def on_device(tokens, grad_out, route_ids, gate_values, gate_proj, up_proj, down_proj):
    tok_rows, features = tokens.shape
    top_count = route_ids.shape[1]
    n_dp = lax.axis_size("dp")
    n_ex = lax.axis_size("expert")
    groups = n_dp * n_ex
    capacity = max(2, tok_rows * top_count * 9 // (8 * groups))
    plane = lax.axis_index("dp")
    core = lax.axis_index("tensor")
    routes = tok_rows * top_count
    block_slots = n_ex * capacity
    lanes = 128

    carried = jnp.where(core == 0, tokens, grad_out)
    aux = jnp.concatenate([route_ids.astype(tokens.dtype), gate_values.astype(tokens.dtype)], axis=1)
    aux = jnp.pad(aux, ((0, 0), (0, lanes - aux.shape[1])))
    ext = jnp.concatenate([carried, aux], axis=1)
    blocks = [ext] + [
        lax.ppermute(ext, "dp", [(i, (i + s) % n_dp) for i in range(n_dp)])
        for s in range(1, n_dp)
    ]

    r_iota = jnp.arange(routes, dtype=jnp.int32)
    earlier = (r_iota[None, :] < r_iota[:, None]).astype(jnp.bfloat16)
    e_iota = jnp.arange(n_ex, dtype=jnp.int32)
    q_iota = jnp.arange(block_slots, dtype=jnp.int32)

    weight_g = gate_proj[0]
    weight_u = up_proj[0]
    weight_d = down_proj[0]
    acc_g = acc_u = acc_d = None
    col_parts = []
    anchors = []
    for s, blk in enumerate(blocks):
        carried_b = blk[:, :features]
        ids_b = blk[:, features:features + top_count].astype(jnp.int32)
        gates_b = blk[:, features + top_count:features + 2 * top_count].astype(jnp.float32)

        local_ex = ids_b.reshape(routes) - plane * n_ex
        in_plane = (local_ex >= 0) & (local_ex < n_ex)
        one_hot = local_ex[:, None] == e_iota[None, :]
        running = jnp.dot(earlier, one_hot.astype(jnp.bfloat16), preferred_element_type=jnp.float32)
        position = jnp.sum(running * one_hot.astype(jnp.float32), axis=1).astype(jnp.int32)
        key = jnp.where(in_plane, local_ex * capacity + position, -1).reshape(tok_rows, top_count)
        match = key[None, :, :] == q_iota[:, None, None]
        select = jnp.sum(match.astype(jnp.bfloat16), axis=2)
        send_rows = jnp.dot(select, carried_b, preferred_element_type=jnp.float32).astype(tokens.dtype)
        send_gate = jnp.sum(jnp.where(match, gates_b[None, :, :], 0.0), axis=(1, 2))
        gate_cols = jnp.pad(send_gate.astype(tokens.dtype)[:, None], ((0, 0), (0, lanes - 1)))
        send = jnp.concatenate([send_rows, gate_cols], axis=1)

        if s >= 2:
            send = lax.optimization_barrier((send, anchors[s - 2]))[0]
        recv = lax.all_to_all(
            send.reshape(n_ex, capacity, features + lanes), "expert", split_axis=0, concat_axis=0, tiled=True
        ).reshape(block_slots, features + lanes)
        both = lax.all_gather(recv, "tensor")
        routed_x = both[0, :, :features]
        routed_dy = both[1, :, :features]
        routed_gate = both[0, :, features]

        gate_pre = jnp.dot(routed_x, weight_g, preferred_element_type=jnp.float32)
        up_pre = jnp.dot(routed_x, weight_u, preferred_element_type=jnp.float32)
        sig_gate = jax.nn.sigmoid(gate_pre)
        silu_gate = gate_pre * sig_gate
        activation = (silu_gate * up_pre).astype(jnp.bfloat16)
        hidden_grad = lax.dot_general(
            routed_dy, weight_d, (((1,), (1,)), ((), ())), preferred_element_type=jnp.float32
        )
        gate_terms = jnp.sum(hidden_grad * activation.astype(jnp.float32), axis=1)
        row_gate = routed_gate.astype(jnp.float32)[:, None]
        scaled = row_gate * hidden_grad
        up_grad = (scaled * silu_gate).astype(jnp.bfloat16)
        pre_grad = (scaled * up_pre * sig_gate * (1.0 + gate_pre * (1.0 - sig_gate))).astype(
            jnp.bfloat16
        )
        anchors.append(pre_grad)
        part_g = lax.dot_general(
            routed_x, pre_grad, (((0,), (0,)), ((), ())), preferred_element_type=jnp.float32
        )
        part_u = lax.dot_general(
            routed_x, up_grad, (((0,), (0,)), ((), ())), preferred_element_type=jnp.float32
        )
        weighted = (row_gate * activation.astype(jnp.float32)).astype(jnp.bfloat16)
        part_d = lax.dot_general(
            weighted, routed_dy, (((0,), (0,)), ((), ())), preferred_element_type=jnp.float32
        )
        if acc_g is None:
            acc_g, acc_u, acc_d = part_g, part_u, part_d
        else:
            acc_g, acc_u, acc_d = acc_g + part_g, acc_u + part_u, acc_d + part_d
        gate_col = jnp.pad(gate_terms[:, None], ((0, 0), (0, lanes - 1)))
        pieces = []
        half = features // 2
        for h in range(2):
            rows = slice(h * half, (h + 1) * half)
            pieces.append(
                lax.dot_general(
                    pre_grad, weight_g[rows], (((1,), (1,)), ((), ())), preferred_element_type=jnp.float32
                ) + lax.dot_general(
                    up_grad, weight_u[rows], (((1,), (1,)), ((), ())), preferred_element_type=jnp.float32
                )
            )
            pieces.append(gate_col)
        ret = lax.psum_scatter(
            jnp.concatenate(pieces, axis=1), "tensor", scatter_dimension=1, tiled=True
        ).astype(jnp.bfloat16)
        back = lax.all_to_all(
            ret.reshape(n_ex, capacity, half + lanes), "expert", split_axis=0, concat_axis=0, tiled=True
        ).reshape(block_slots, half + lanes)

        col_grad = lax.dot_general(
            select, back[:, :half], (((0,), (0,)), ((), ())), preferred_element_type=jnp.float32
        )
        col_gate = jnp.sum(
            jnp.where(match, back[:, half].astype(jnp.float32)[:, None, None], 0.0), axis=0
        )
        part = jnp.concatenate(
            [col_grad, jnp.pad(col_gate, ((0, 0), (0, lanes - top_count)))], axis=1
        ).astype(jnp.bfloat16)
        if s:
            part = lax.ppermute(part, "dp", [(i, (i - s) % n_dp) for i in range(n_dp)])
        col_parts.append(part.astype(jnp.float32))

    total = sum(col_parts[1:], col_parts[0])
    half = total.shape[1] - lanes
    token_grad = total[:, :half].astype(jnp.bfloat16)
    gate_grad = total[:, half:half + top_count].astype(jnp.bfloat16)
    grad_g = acc_g.astype(jnp.bfloat16)
    grad_u = acc_u.astype(jnp.bfloat16)
    grad_d = acc_d.astype(jnp.bfloat16)
    return (token_grad, gate_grad, grad_g[None], grad_u[None], grad_d[None])


def solution(mesh):
    in_specs = (
        P(("dp", "expert"), None),
        P(("dp", "expert"), None),
        P(("dp", "expert"), None),
        P(("dp", "expert"), None),
        P(("dp", "expert"), None, "tensor"),
        P(("dp", "expert"), None, "tensor"),
        P(("dp", "expert"), "tensor", None),
    )
    out_specs = (
        P(("dp", "expert"), "tensor"),
        P(("dp", "expert"), None),
        P(("dp", "expert"), None, "tensor"),
        P(("dp", "expert"), None, "tensor"),
        P(("dp", "expert"), "tensor", None),
    )
    return jax.shard_map(
        on_device, mesh=mesh, in_specs=in_specs, out_specs=out_specs, check_vma=False
    )
```

```python
import jax
import jax.numpy as jnp
from jax import lax
from jax.sharding import PartitionSpec as P


def on_device(tokens, grad_out, route_ids, gate_values, gate_proj, up_proj, down_proj):
    tok_rows, features = tokens.shape
    top_count = route_ids.shape[1]
    n_dp = lax.axis_size("dp")
    n_ex = lax.axis_size("expert")
    groups = n_dp * n_ex
    capacity = max(2, tok_rows * top_count * 9 // (8 * groups))
    plane = lax.axis_index("dp")
    core = lax.axis_index("tensor")
    routes = tok_rows * top_count
    block_slots = n_ex * capacity
    lanes = 128

    carried = jnp.where(core == 0, tokens, grad_out)
    aux = jnp.concatenate([route_ids.astype(tokens.dtype), gate_values.astype(tokens.dtype)], axis=1)
    aux = jnp.pad(aux, ((0, 0), (0, lanes - aux.shape[1])))
    ext = jnp.concatenate([carried, aux], axis=1)
    blocks = [ext] + [
        lax.ppermute(ext, "dp", [(i, (i + s) % n_dp) for i in range(n_dp)])
        for s in range(1, n_dp)
    ]

    r_iota = jnp.arange(routes, dtype=jnp.int32)
    earlier = (r_iota[None, :] < r_iota[:, None]).astype(jnp.bfloat16)
    e_iota = jnp.arange(n_ex, dtype=jnp.int32)
    q_iota = jnp.arange(block_slots, dtype=jnp.int32)

    weight_g = gate_proj[0]
    weight_u = up_proj[0]
    weight_d = down_proj[0]
    rows_x, rows_dy, rows_pre, rows_up, rows_w = [], [], [], [], []
    col_parts = []
    anchors = []
    for s, blk in enumerate(blocks):
        carried_b = blk[:, :features]
        ids_b = blk[:, features:features + top_count].astype(jnp.int32)
        gates_b = blk[:, features + top_count:features + 2 * top_count].astype(jnp.float32)

        local_ex = ids_b.reshape(routes) - plane * n_ex
        in_plane = (local_ex >= 0) & (local_ex < n_ex)
        one_hot = local_ex[:, None] == e_iota[None, :]
        running = jnp.dot(earlier, one_hot.astype(jnp.bfloat16), preferred_element_type=jnp.float32)
        position = jnp.sum(running * one_hot.astype(jnp.float32), axis=1).astype(jnp.int32)
        key = jnp.where(in_plane, local_ex * capacity + position, -1).reshape(tok_rows, top_count)
        match = key[None, :, :] == q_iota[:, None, None]
        select = jnp.sum(match.astype(jnp.bfloat16), axis=2)
        send_rows = jnp.dot(select, carried_b, preferred_element_type=jnp.float32).astype(tokens.dtype)
        send_gate = jnp.sum(jnp.where(match, gates_b[None, :, :], 0.0), axis=(1, 2))
        gate_cols = jnp.pad(send_gate.astype(tokens.dtype)[:, None], ((0, 0), (0, lanes - 1)))
        send = jnp.concatenate([send_rows, gate_cols], axis=1)

        if s >= 2:
            send = lax.optimization_barrier((send, anchors[s - 2]))[0]
        recv = lax.all_to_all(
            send.reshape(n_ex, capacity, features + lanes), "expert", split_axis=0, concat_axis=0, tiled=True
        ).reshape(block_slots, features + lanes)
        both = lax.all_gather(recv, "tensor")
        routed_x = both[0, :, :features]
        routed_dy = both[1, :, :features]
        routed_gate = both[0, :, features]

        gate_pre = jnp.dot(routed_x, weight_g, preferred_element_type=jnp.float32)
        up_pre = jnp.dot(routed_x, weight_u, preferred_element_type=jnp.float32)
        sig_gate = jax.nn.sigmoid(gate_pre)
        silu_gate = gate_pre * sig_gate
        activation = (silu_gate * up_pre).astype(jnp.bfloat16)
        hidden_grad = lax.dot_general(
            routed_dy, weight_d, (((1,), (1,)), ((), ())), preferred_element_type=jnp.float32
        )
        gate_terms = jnp.sum(hidden_grad * activation.astype(jnp.float32), axis=1)
        row_gate = routed_gate.astype(jnp.float32)[:, None]
        scaled = row_gate * hidden_grad
        up_grad = (scaled * silu_gate).astype(jnp.bfloat16)
        pre_grad = (scaled * up_pre * sig_gate * (1.0 + gate_pre * (1.0 - sig_gate))).astype(
            jnp.bfloat16
        )
        anchors.append(pre_grad)
        weighted = (row_gate * activation.astype(jnp.float32)).astype(jnp.bfloat16)
        rows_x.append(routed_x)
        rows_dy.append(routed_dy)
        rows_pre.append(pre_grad)
        rows_up.append(up_grad)
        rows_w.append(weighted)
        gate_col = jnp.pad(gate_terms[:, None], ((0, 0), (0, lanes - 1)))
        pieces = []
        half = features // 2
        for h in range(2):
            rows = slice(h * half, (h + 1) * half)
            pieces.append(
                lax.dot_general(
                    pre_grad, weight_g[rows], (((1,), (1,)), ((), ())), preferred_element_type=jnp.float32
                ) + lax.dot_general(
                    up_grad, weight_u[rows], (((1,), (1,)), ((), ())), preferred_element_type=jnp.float32
                )
            )
            pieces.append(gate_col)
        ret = lax.psum_scatter(
            jnp.concatenate(pieces, axis=1), "tensor", scatter_dimension=1, tiled=True
        ).astype(jnp.bfloat16)
        back = lax.all_to_all(
            ret.reshape(n_ex, capacity, half + lanes), "expert", split_axis=0, concat_axis=0, tiled=True
        ).reshape(block_slots, half + lanes)

        col_grad = lax.dot_general(
            select, back[:, :half], (((0,), (0,)), ((), ())), preferred_element_type=jnp.float32
        )
        col_gate = jnp.sum(
            jnp.where(match, back[:, half].astype(jnp.float32)[:, None, None], 0.0), axis=0
        )
        part = jnp.concatenate(
            [col_grad, jnp.pad(col_gate, ((0, 0), (0, lanes - top_count)))], axis=1
        ).astype(jnp.bfloat16)
        if s:
            part = lax.ppermute(part, "dp", [(i, (i - s) % n_dp) for i in range(n_dp)])
        col_parts.append(part.astype(jnp.float32))

    total = sum(col_parts[1:], col_parts[0])
    half = total.shape[1] - lanes
    token_grad = total[:, :half].astype(jnp.bfloat16)
    gate_grad = total[:, half:half + top_count].astype(jnp.bfloat16)
    all_x = jnp.concatenate(rows_x, axis=0)
    all_dy = jnp.concatenate(rows_dy, axis=0)
    grad_g = lax.dot_general(
        all_x, jnp.concatenate(rows_pre, axis=0), (((0,), (0,)), ((), ())),
        preferred_element_type=jnp.float32,
    ).astype(jnp.bfloat16)
    grad_u = lax.dot_general(
        all_x, jnp.concatenate(rows_up, axis=0), (((0,), (0,)), ((), ())),
        preferred_element_type=jnp.float32,
    ).astype(jnp.bfloat16)
    grad_d = lax.dot_general(
        jnp.concatenate(rows_w, axis=0), all_dy, (((0,), (0,)), ((), ())),
        preferred_element_type=jnp.float32,
    ).astype(jnp.bfloat16)
    return (token_grad, gate_grad, grad_g[None], grad_u[None], grad_d[None])


def solution(mesh):
    in_specs = (
        P(("dp", "expert"), None),
        P(("dp", "expert"), None),
        P(("dp", "expert"), None),
        P(("dp", "expert"), None),
        P(("dp", "expert"), None, "tensor"),
        P(("dp", "expert"), None, "tensor"),
        P(("dp", "expert"), "tensor", None),
    )
    out_specs = (
        P(("dp", "expert"), "tensor"),
        P(("dp", "expert"), None),
        P(("dp", "expert"), None, "tensor"),
        P(("dp", "expert"), None, "tensor"),
        P(("dp", "expert"), "tensor", None),
    )
    return jax.shard_map(
        on_device, mesh=mesh, in_specs=in_specs, out_specs=out_specs, check_vma=False
    )
```

```python
import jax
import jax.numpy as jnp
from jax import lax
from jax.sharding import PartitionSpec as P


def on_device(tokens, grad_out, route_ids, gate_values, gate_proj, up_proj, down_proj):
    tok_rows, features = tokens.shape
    top_count = route_ids.shape[1]
    n_dp = lax.axis_size("dp")
    n_ex = lax.axis_size("expert")
    groups = n_dp * n_ex
    capacity = max(2, tok_rows * top_count * 9 // (8 * groups))
    plane = lax.axis_index("dp")
    core = lax.axis_index("tensor")
    routes = tok_rows * top_count
    block_slots = n_ex * capacity
    lanes = 128

    carried = jnp.where(core == 0, tokens, grad_out)
    aux = jnp.concatenate([route_ids.astype(tokens.dtype), gate_values.astype(tokens.dtype)], axis=1)
    aux = jnp.pad(aux, ((0, 0), (0, lanes - aux.shape[1])))
    ext = jnp.concatenate([carried, aux], axis=1)
    blocks = [ext] + [
        lax.ppermute(ext, "dp", [(i, (i + s) % n_dp) for i in range(n_dp)])
        for s in range(1, n_dp)
    ]

    r_iota = jnp.arange(routes, dtype=jnp.int32)
    earlier = (r_iota[None, :] < r_iota[:, None]).astype(jnp.bfloat16)
    e_iota = jnp.arange(n_ex, dtype=jnp.int32)
    q_iota = jnp.arange(block_slots, dtype=jnp.int32)

    weight_g = gate_proj[0]
    weight_u = up_proj[0]
    weight_d = down_proj[0]
    rows_x, rows_dy, rows_pre, rows_up, rows_w = [], [], [], [], []
    col_parts = []
    anchors = []
    backs = []
    for s, blk in enumerate(blocks):
        carried_b = blk[:, :features]
        ids_b = blk[:, features:features + top_count].astype(jnp.int32)
        gates_b = blk[:, features + top_count:features + 2 * top_count].astype(jnp.float32)

        local_ex = ids_b.reshape(routes) - plane * n_ex
        in_plane = (local_ex >= 0) & (local_ex < n_ex)
        one_hot = local_ex[:, None] == e_iota[None, :]
        running = jnp.dot(earlier, one_hot.astype(jnp.bfloat16), preferred_element_type=jnp.float32)
        position = jnp.sum(running * one_hot.astype(jnp.float32), axis=1).astype(jnp.int32)
        key = jnp.where(in_plane, local_ex * capacity + position, -1).reshape(tok_rows, top_count)
        match = key[None, :, :] == q_iota[:, None, None]
        select = jnp.sum(match.astype(jnp.bfloat16), axis=2)
        send_rows = jnp.dot(select, carried_b, preferred_element_type=jnp.float32).astype(tokens.dtype)
        send_gate = jnp.sum(jnp.where(match, gates_b[None, :, :], 0.0), axis=(1, 2))
        gate_cols = jnp.pad(send_gate.astype(tokens.dtype)[:, None], ((0, 0), (0, lanes - 1)))
        send = jnp.concatenate([send_rows, gate_cols], axis=1)

        if s >= 2:
            send = lax.optimization_barrier((send, anchors[s - 2]))[0]
        recv = lax.all_to_all(
            send.reshape(n_ex, capacity, features + lanes), "expert", split_axis=0, concat_axis=0, tiled=True
        ).reshape(block_slots, features + lanes)
        if s >= 2:
            recv = lax.optimization_barrier((recv, backs[s - 2]))[0]
        both = lax.all_gather(recv, "tensor")
        routed_x = both[0, :, :features]
        routed_dy = both[1, :, :features]
        routed_gate = both[0, :, features]

        gate_pre = jnp.dot(routed_x, weight_g, preferred_element_type=jnp.float32)
        up_pre = jnp.dot(routed_x, weight_u, preferred_element_type=jnp.float32)
        sig_gate = jax.nn.sigmoid(gate_pre)
        silu_gate = gate_pre * sig_gate
        activation = (silu_gate * up_pre).astype(jnp.bfloat16)
        hidden_grad = lax.dot_general(
            routed_dy, weight_d, (((1,), (1,)), ((), ())), preferred_element_type=jnp.float32
        )
        gate_terms = jnp.sum(hidden_grad * activation.astype(jnp.float32), axis=1)
        row_gate = routed_gate.astype(jnp.float32)[:, None]
        scaled = row_gate * hidden_grad
        up_grad = (scaled * silu_gate).astype(jnp.bfloat16)
        pre_grad = (scaled * up_pre * sig_gate * (1.0 + gate_pre * (1.0 - sig_gate))).astype(
            jnp.bfloat16
        )
        anchors.append(pre_grad)
        weighted = (row_gate * activation.astype(jnp.float32)).astype(jnp.bfloat16)
        rows_x.append(routed_x)
        rows_dy.append(routed_dy)
        rows_pre.append(pre_grad)
        rows_up.append(up_grad)
        rows_w.append(weighted)
        gate_col = jnp.pad(gate_terms[:, None], ((0, 0), (0, lanes - 1)))
        pieces = []
        half = features // 2
        for h in range(2):
            rows = slice(h * half, (h + 1) * half)
            pieces.append(
                lax.dot_general(
                    pre_grad, weight_g[rows], (((1,), (1,)), ((), ())), preferred_element_type=jnp.float32
                ) + lax.dot_general(
                    up_grad, weight_u[rows], (((1,), (1,)), ((), ())), preferred_element_type=jnp.float32
                )
            )
            pieces.append(gate_col)
        ret = lax.psum_scatter(
            jnp.concatenate(pieces, axis=1), "tensor", scatter_dimension=1, tiled=True
        ).astype(jnp.bfloat16)
        back = lax.all_to_all(
            ret.reshape(n_ex, capacity, half + lanes), "expert", split_axis=0, concat_axis=0, tiled=True
        ).reshape(block_slots, half + lanes)
        backs.append(back)

        col_grad = lax.dot_general(
            select, back[:, :half], (((0,), (0,)), ((), ())), preferred_element_type=jnp.float32
        )
        col_gate = jnp.sum(
            jnp.where(match, back[:, half].astype(jnp.float32)[:, None, None], 0.0), axis=0
        )
        part = jnp.concatenate(
            [col_grad, jnp.pad(col_gate, ((0, 0), (0, lanes - top_count)))], axis=1
        ).astype(jnp.bfloat16)
        if s:
            part = lax.ppermute(part, "dp", [(i, (i - s) % n_dp) for i in range(n_dp)])
        col_parts.append(part.astype(jnp.float32))

    total = sum(col_parts[1:], col_parts[0])
    half = total.shape[1] - lanes
    token_grad = total[:, :half].astype(jnp.bfloat16)
    gate_grad = total[:, half:half + top_count].astype(jnp.bfloat16)
    all_x = jnp.concatenate(rows_x, axis=0)
    all_dy = jnp.concatenate(rows_dy, axis=0)
    grad_g = lax.dot_general(
        all_x, jnp.concatenate(rows_pre, axis=0), (((0,), (0,)), ((), ())),
        preferred_element_type=jnp.float32,
    ).astype(jnp.bfloat16)
    grad_u = lax.dot_general(
        all_x, jnp.concatenate(rows_up, axis=0), (((0,), (0,)), ((), ())),
        preferred_element_type=jnp.float32,
    ).astype(jnp.bfloat16)
    grad_d = lax.dot_general(
        jnp.concatenate(rows_w, axis=0), all_dy, (((0,), (0,)), ((), ())),
        preferred_element_type=jnp.float32,
    ).astype(jnp.bfloat16)
    return (token_grad, gate_grad, grad_g[None], grad_u[None], grad_d[None])


def solution(mesh):
    in_specs = (
        P(("dp", "expert"), None),
        P(("dp", "expert"), None),
        P(("dp", "expert"), None),
        P(("dp", "expert"), None),
        P(("dp", "expert"), None, "tensor"),
        P(("dp", "expert"), None, "tensor"),
        P(("dp", "expert"), "tensor", None),
    )
    out_specs = (
        P(("dp", "expert"), "tensor"),
        P(("dp", "expert"), None),
        P(("dp", "expert"), None, "tensor"),
        P(("dp", "expert"), None, "tensor"),
        P(("dp", "expert"), "tensor", None),
    )
    return jax.shard_map(
        on_device, mesh=mesh, in_specs=in_specs, out_specs=out_specs, check_vma=False
    )
```

```python
import jax
import jax.numpy as jnp
from jax import lax
from jax.sharding import PartitionSpec as P


def on_device(tokens, grad_out, route_ids, gate_values, gate_proj, up_proj, down_proj):
    tok_rows, features = tokens.shape
    top_count = route_ids.shape[1]
    n_dp = lax.axis_size("dp")
    n_ex = lax.axis_size("expert")
    groups = n_dp * n_ex
    capacity = max(2, tok_rows * top_count * 9 // (8 * groups))
    plane = lax.axis_index("dp")
    core = lax.axis_index("tensor")
    routes = tok_rows * top_count
    block_slots = n_ex * capacity
    lanes = 128

    carried = jnp.where(core == 0, tokens, grad_out)
    aux = jnp.concatenate([route_ids.astype(tokens.dtype), gate_values.astype(tokens.dtype)], axis=1)
    aux = jnp.pad(aux, ((0, 0), (0, lanes - aux.shape[1])))
    ext = jnp.concatenate([carried, aux], axis=1)
    blocks = [ext]
    for s in range(1, n_dp):
        source = ext if s == 1 else lax.optimization_barrier((ext, blocks[-1]))[0]
        blocks.append(lax.ppermute(source, "dp", [(i, (i + s) % n_dp) for i in range(n_dp)]))

    r_iota = jnp.arange(routes, dtype=jnp.int32)
    earlier = (r_iota[None, :] < r_iota[:, None]).astype(jnp.bfloat16)
    e_iota = jnp.arange(n_ex, dtype=jnp.int32)
    q_iota = jnp.arange(block_slots, dtype=jnp.int32)

    weight_g = gate_proj[0]
    weight_u = up_proj[0]
    weight_d = down_proj[0]
    rows_x, rows_dy, rows_pre, rows_up, rows_w = [], [], [], [], []
    col_parts = []
    anchors = []
    for s, blk in enumerate(blocks):
        if s == 1:
            blk = lax.optimization_barrier((blk, anchors[0]))[0]
        carried_b = blk[:, :features]
        ids_b = blk[:, features:features + top_count].astype(jnp.int32)
        gates_b = blk[:, features + top_count:features + 2 * top_count].astype(jnp.float32)

        local_ex = ids_b.reshape(routes) - plane * n_ex
        in_plane = (local_ex >= 0) & (local_ex < n_ex)
        one_hot = local_ex[:, None] == e_iota[None, :]
        running = jnp.dot(earlier, one_hot.astype(jnp.bfloat16), preferred_element_type=jnp.float32)
        position = jnp.sum(running * one_hot.astype(jnp.float32), axis=1).astype(jnp.int32)
        key = jnp.where(in_plane, local_ex * capacity + position, -1).reshape(tok_rows, top_count)
        match = key[None, :, :] == q_iota[:, None, None]
        select = jnp.sum(match.astype(jnp.bfloat16), axis=2)
        send_rows = jnp.dot(select, carried_b, preferred_element_type=jnp.float32).astype(tokens.dtype)
        send_gate = jnp.sum(jnp.where(match, gates_b[None, :, :], 0.0), axis=(1, 2))
        gate_cols = jnp.pad(send_gate.astype(tokens.dtype)[:, None], ((0, 0), (0, lanes - 1)))
        send = jnp.concatenate([send_rows, gate_cols], axis=1)

        if s >= 2:
            send = lax.optimization_barrier((send, anchors[s - 2]))[0]
        recv = lax.all_to_all(
            send.reshape(n_ex, capacity, features + lanes), "expert", split_axis=0, concat_axis=0, tiled=True
        ).reshape(block_slots, features + lanes)
        both = lax.all_gather(recv, "tensor")
        routed_x = both[0, :, :features]
        routed_dy = both[1, :, :features]
        routed_gate = both[0, :, features]

        gate_pre = jnp.dot(routed_x, weight_g, preferred_element_type=jnp.float32)
        up_pre = jnp.dot(routed_x, weight_u, preferred_element_type=jnp.float32)
        sig_gate = jax.nn.sigmoid(gate_pre)
        silu_gate = gate_pre * sig_gate
        activation = (silu_gate * up_pre).astype(jnp.bfloat16)
        hidden_grad = lax.dot_general(
            routed_dy, weight_d, (((1,), (1,)), ((), ())), preferred_element_type=jnp.float32
        )
        gate_terms = jnp.sum(hidden_grad * activation.astype(jnp.float32), axis=1)
        row_gate = routed_gate.astype(jnp.float32)[:, None]
        scaled = row_gate * hidden_grad
        up_grad = (scaled * silu_gate).astype(jnp.bfloat16)
        pre_grad = (scaled * up_pre * sig_gate * (1.0 + gate_pre * (1.0 - sig_gate))).astype(
            jnp.bfloat16
        )
        anchors.append(pre_grad)
        weighted = (row_gate * activation.astype(jnp.float32)).astype(jnp.bfloat16)
        rows_x.append(routed_x)
        rows_dy.append(routed_dy)
        rows_pre.append(pre_grad)
        rows_up.append(up_grad)
        rows_w.append(weighted)
        gate_col = jnp.pad(gate_terms[:, None], ((0, 0), (0, lanes - 1)))
        pieces = []
        half = features // 2
        for h in range(2):
            rows = slice(h * half, (h + 1) * half)
            pieces.append(
                lax.dot_general(
                    pre_grad, weight_g[rows], (((1,), (1,)), ((), ())), preferred_element_type=jnp.float32
                ) + lax.dot_general(
                    up_grad, weight_u[rows], (((1,), (1,)), ((), ())), preferred_element_type=jnp.float32
                )
            )
            pieces.append(gate_col)
        ret = lax.psum_scatter(
            jnp.concatenate(pieces, axis=1), "tensor", scatter_dimension=1, tiled=True
        ).astype(jnp.bfloat16)
        back = lax.all_to_all(
            ret.reshape(n_ex, capacity, half + lanes), "expert", split_axis=0, concat_axis=0, tiled=True
        ).reshape(block_slots, half + lanes)

        col_grad = lax.dot_general(
            select, back[:, :half], (((0,), (0,)), ((), ())), preferred_element_type=jnp.float32
        )
        col_gate = jnp.sum(
            jnp.where(match, back[:, half].astype(jnp.float32)[:, None, None], 0.0), axis=0
        )
        part = jnp.concatenate(
            [col_grad, jnp.pad(col_gate, ((0, 0), (0, lanes - top_count)))], axis=1
        ).astype(jnp.bfloat16)
        if s:
            part = lax.ppermute(part, "dp", [(i, (i - s) % n_dp) for i in range(n_dp)])
        col_parts.append(part.astype(jnp.float32))

    total = sum(col_parts[1:], col_parts[0])
    half = total.shape[1] - lanes
    token_grad = total[:, :half].astype(jnp.bfloat16)
    gate_grad = total[:, half:half + top_count].astype(jnp.bfloat16)
    all_x = jnp.concatenate(rows_x, axis=0)
    all_dy = jnp.concatenate(rows_dy, axis=0)
    grad_g = lax.dot_general(
        all_x, jnp.concatenate(rows_pre, axis=0), (((0,), (0,)), ((), ())),
        preferred_element_type=jnp.float32,
    ).astype(jnp.bfloat16)
    grad_u = lax.dot_general(
        all_x, jnp.concatenate(rows_up, axis=0), (((0,), (0,)), ((), ())),
        preferred_element_type=jnp.float32,
    ).astype(jnp.bfloat16)
    grad_d = lax.dot_general(
        jnp.concatenate(rows_w, axis=0), all_dy, (((0,), (0,)), ((), ())),
        preferred_element_type=jnp.float32,
    ).astype(jnp.bfloat16)
    return (token_grad, gate_grad, grad_g[None], grad_u[None], grad_d[None])


def solution(mesh):
    in_specs = (
        P(("dp", "expert"), None),
        P(("dp", "expert"), None),
        P(("dp", "expert"), None),
        P(("dp", "expert"), None),
        P(("dp", "expert"), None, "tensor"),
        P(("dp", "expert"), None, "tensor"),
        P(("dp", "expert"), "tensor", None),
    )
    out_specs = (
        P(("dp", "expert"), "tensor"),
        P(("dp", "expert"), None),
        P(("dp", "expert"), None, "tensor"),
        P(("dp", "expert"), None, "tensor"),
        P(("dp", "expert"), "tensor", None),
    )
    return jax.shard_map(
        on_device, mesh=mesh, in_specs=in_specs, out_specs=out_specs, check_vma=False
    )
```

```python
import jax
import jax.numpy as jnp
from jax import lax
from jax.sharding import PartitionSpec as P


def on_device(tokens, grad_out, route_ids, gate_values, gate_proj, up_proj, down_proj):
    tok_rows, features = tokens.shape
    top_count = route_ids.shape[1]
    n_dp = lax.axis_size("dp")
    n_ex = lax.axis_size("expert")
    groups = n_dp * n_ex
    capacity = max(2, tok_rows * top_count * 9 // (8 * groups))
    plane = lax.axis_index("dp")
    core = lax.axis_index("tensor")
    routes = tok_rows * top_count
    block_slots = n_ex * capacity
    lanes = 128

    carried = jnp.where(core == 0, tokens, grad_out)
    aux = jnp.concatenate([route_ids.astype(tokens.dtype), gate_values.astype(tokens.dtype)], axis=1)
    aux = jnp.pad(aux, ((0, 0), (0, lanes - aux.shape[1])))
    ext = jnp.concatenate([carried, aux], axis=1)
    blocks = [ext] + [
        lax.ppermute(ext, "dp", [(i, (i + s) % n_dp) for i in range(n_dp)])
        for s in range(1, n_dp)
    ]

    r_iota = jnp.arange(routes, dtype=jnp.int32)
    earlier = (r_iota[None, :] < r_iota[:, None]).astype(jnp.bfloat16)
    e_iota = jnp.arange(n_ex, dtype=jnp.int32)
    q_iota = jnp.arange(block_slots, dtype=jnp.int32)

    weight_g = gate_proj[0]
    weight_u = up_proj[0]
    weight_d = down_proj[0]
    rows_x, rows_dy, rows_pre, rows_up, rows_w = [], [], [], [], []
    col_parts = []
    anchors = []
    pair = 2 if n_dp % 2 == 0 else 1
    groups_of = [list(range(g, g + pair)) for g in range(0, n_dp, pair)]
    for gi, members in enumerate(groups_of):
        sends, selects, matches = [], [], []
        for s in members:
            blk = blocks[s]
            carried_b = blk[:, :features]
            ids_b = blk[:, features:features + top_count].astype(jnp.int32)
            gates_b = blk[:, features + top_count:features + 2 * top_count].astype(jnp.float32)

            local_ex = ids_b.reshape(routes) - plane * n_ex
            in_plane = (local_ex >= 0) & (local_ex < n_ex)
            one_hot = local_ex[:, None] == e_iota[None, :]
            running = jnp.dot(earlier, one_hot.astype(jnp.bfloat16), preferred_element_type=jnp.float32)
            position = jnp.sum(running * one_hot.astype(jnp.float32), axis=1).astype(jnp.int32)
            key = jnp.where(in_plane, local_ex * capacity + position, -1).reshape(tok_rows, top_count)
            match = key[None, :, :] == q_iota[:, None, None]
            select = jnp.sum(match.astype(jnp.bfloat16), axis=2)
            send_rows = jnp.dot(select, carried_b, preferred_element_type=jnp.float32).astype(tokens.dtype)
            send_gate = jnp.sum(jnp.where(match, gates_b[None, :, :], 0.0), axis=(1, 2))
            gate_cols = jnp.pad(send_gate.astype(tokens.dtype)[:, None], ((0, 0), (0, lanes - 1)))
            sends.append(jnp.concatenate([send_rows, gate_cols], axis=1))
            selects.append(select)
            matches.append(match)
        send = jnp.stack(sends)
        n_mem = len(members)

        if gi >= 2:
            send = lax.optimization_barrier((send, anchors[gi - 2]))[0]
        recv = lax.all_to_all(
            send.reshape(n_mem, n_ex, capacity, features + lanes), "expert", split_axis=1, concat_axis=1, tiled=True
        ).reshape(n_mem * block_slots, features + lanes)
        both = lax.all_gather(recv, "tensor")
        routed_x = both[0, :, :features]
        routed_dy = both[1, :, :features]
        routed_gate = both[0, :, features]

        gate_pre = jnp.dot(routed_x, weight_g, preferred_element_type=jnp.float32)
        up_pre = jnp.dot(routed_x, weight_u, preferred_element_type=jnp.float32)
        sig_gate = jax.nn.sigmoid(gate_pre)
        silu_gate = gate_pre * sig_gate
        activation = (silu_gate * up_pre).astype(jnp.bfloat16)
        hidden_grad = lax.dot_general(
            routed_dy, weight_d, (((1,), (1,)), ((), ())), preferred_element_type=jnp.float32
        )
        gate_terms = jnp.sum(hidden_grad * activation.astype(jnp.float32), axis=1)
        row_gate = routed_gate.astype(jnp.float32)[:, None]
        scaled = row_gate * hidden_grad
        up_grad = (scaled * silu_gate).astype(jnp.bfloat16)
        pre_grad = (scaled * up_pre * sig_gate * (1.0 + gate_pre * (1.0 - sig_gate))).astype(
            jnp.bfloat16
        )
        anchors.append(pre_grad)
        weighted = (row_gate * activation.astype(jnp.float32)).astype(jnp.bfloat16)
        rows_x.append(routed_x)
        rows_dy.append(routed_dy)
        rows_pre.append(pre_grad)
        rows_up.append(up_grad)
        rows_w.append(weighted)
        gate_col = jnp.pad(gate_terms[:, None], ((0, 0), (0, lanes - 1)))
        pieces = []
        half = features // 2
        for h in range(2):
            rows = slice(h * half, (h + 1) * half)
            pieces.append(
                lax.dot_general(
                    pre_grad, weight_g[rows], (((1,), (1,)), ((), ())), preferred_element_type=jnp.float32
                ) + lax.dot_general(
                    up_grad, weight_u[rows], (((1,), (1,)), ((), ())), preferred_element_type=jnp.float32
                )
            )
            pieces.append(gate_col)
        ret = lax.psum_scatter(
            jnp.concatenate(pieces, axis=1), "tensor", scatter_dimension=1, tiled=True
        ).astype(jnp.bfloat16)
        back = lax.all_to_all(
            ret.reshape(n_mem, n_ex, capacity, half + lanes), "expert", split_axis=1, concat_axis=1, tiled=True
        ).reshape(n_mem, block_slots, half + lanes)

        for m, s in enumerate(members):
            col_grad = lax.dot_general(
                selects[m], back[m, :, :half], (((0,), (0,)), ((), ())), preferred_element_type=jnp.float32
            )
            col_gate = jnp.sum(
                jnp.where(matches[m], back[m, :, half].astype(jnp.float32)[:, None, None], 0.0), axis=0
            )
            part = jnp.concatenate(
                [col_grad, jnp.pad(col_gate, ((0, 0), (0, lanes - top_count)))], axis=1
            ).astype(jnp.bfloat16)
            if s:
                part = lax.ppermute(part, "dp", [(i, (i - s) % n_dp) for i in range(n_dp)])
            col_parts.append(part.astype(jnp.float32))

    total = sum(col_parts[1:], col_parts[0])
    half = total.shape[1] - lanes
    token_grad = total[:, :half].astype(jnp.bfloat16)
    gate_grad = total[:, half:half + top_count].astype(jnp.bfloat16)
    all_x = jnp.concatenate(rows_x, axis=0)
    all_dy = jnp.concatenate(rows_dy, axis=0)
    grad_g = lax.dot_general(
        all_x, jnp.concatenate(rows_pre, axis=0), (((0,), (0,)), ((), ())),
        preferred_element_type=jnp.float32,
    ).astype(jnp.bfloat16)
    grad_u = lax.dot_general(
        all_x, jnp.concatenate(rows_up, axis=0), (((0,), (0,)), ((), ())),
        preferred_element_type=jnp.float32,
    ).astype(jnp.bfloat16)
    grad_d = lax.dot_general(
        jnp.concatenate(rows_w, axis=0), all_dy, (((0,), (0,)), ((), ())),
        preferred_element_type=jnp.float32,
    ).astype(jnp.bfloat16)
    return (token_grad, gate_grad, grad_g[None], grad_u[None], grad_d[None])


def solution(mesh):
    in_specs = (
        P(("dp", "expert"), None),
        P(("dp", "expert"), None),
        P(("dp", "expert"), None),
        P(("dp", "expert"), None),
        P(("dp", "expert"), None, "tensor"),
        P(("dp", "expert"), None, "tensor"),
        P(("dp", "expert"), "tensor", None),
    )
    out_specs = (
        P(("dp", "expert"), "tensor"),
        P(("dp", "expert"), None),
        P(("dp", "expert"), None, "tensor"),
        P(("dp", "expert"), None, "tensor"),
        P(("dp", "expert"), "tensor", None),
    )
    return jax.shard_map(
        on_device, mesh=mesh, in_specs=in_specs, out_specs=out_specs, check_vma=False
    )
```

```python
import jax
import jax.numpy as jnp
from jax import lax
from jax.sharding import PartitionSpec as P


def on_device(tokens, grad_out, route_ids, gate_values, gate_proj, up_proj, down_proj):
    tok_rows, features = tokens.shape
    top_count = route_ids.shape[1]
    n_dp = lax.axis_size("dp")
    n_ex = lax.axis_size("expert")
    groups = n_dp * n_ex
    capacity = max(2, tok_rows * top_count * 9 // (8 * groups))
    plane = lax.axis_index("dp")
    core = lax.axis_index("tensor")
    routes = tok_rows * top_count
    block_slots = n_ex * capacity
    lanes = 128

    carried = jnp.where(core == 0, tokens, grad_out)
    aux = jnp.concatenate([route_ids.astype(tokens.dtype), gate_values.astype(tokens.dtype)], axis=1)
    aux = jnp.pad(aux, ((0, 0), (0, lanes - aux.shape[1])))
    ext = jnp.concatenate([carried, aux], axis=1)
    blocks = [ext] + [
        lax.ppermute(ext, "dp", [(i, (i + s) % n_dp) for i in range(n_dp)])
        for s in range(1, n_dp)
    ]

    r_iota = jnp.arange(routes, dtype=jnp.int32)
    earlier = (r_iota[None, :] < r_iota[:, None]).astype(jnp.bfloat16)
    e_iota = jnp.arange(n_ex, dtype=jnp.int32)
    q_iota = jnp.arange(block_slots, dtype=jnp.int32)

    weight_g = gate_proj[0]
    weight_u = up_proj[0]
    weight_d = down_proj[0]
    rows_x, rows_dy, rows_pre, rows_up, rows_w = [], [], [], [], []
    col_parts = []
    anchors = []
    groups_of = [[0]] + ([list(range(1, n_dp))] if n_dp > 1 else [])
    for gi, members in enumerate(groups_of):
        sends, selects, matches = [], [], []
        for s in members:
            blk = blocks[s]
            carried_b = blk[:, :features]
            ids_b = blk[:, features:features + top_count].astype(jnp.int32)
            gates_b = blk[:, features + top_count:features + 2 * top_count].astype(jnp.float32)

            local_ex = ids_b.reshape(routes) - plane * n_ex
            in_plane = (local_ex >= 0) & (local_ex < n_ex)
            one_hot = local_ex[:, None] == e_iota[None, :]
            running = jnp.dot(earlier, one_hot.astype(jnp.bfloat16), preferred_element_type=jnp.float32)
            position = jnp.sum(running * one_hot.astype(jnp.float32), axis=1).astype(jnp.int32)
            key = jnp.where(in_plane, local_ex * capacity + position, -1).reshape(tok_rows, top_count)
            match = key[None, :, :] == q_iota[:, None, None]
            select = jnp.sum(match.astype(jnp.bfloat16), axis=2)
            send_rows = jnp.dot(select, carried_b, preferred_element_type=jnp.float32).astype(tokens.dtype)
            send_gate = jnp.sum(jnp.where(match, gates_b[None, :, :], 0.0), axis=(1, 2))
            gate_cols = jnp.pad(send_gate.astype(tokens.dtype)[:, None], ((0, 0), (0, lanes - 1)))
            sends.append(jnp.concatenate([send_rows, gate_cols], axis=1))
            selects.append(select)
            matches.append(match)
        send = jnp.stack(sends)
        n_mem = len(members)

        if gi >= 2:
            send = lax.optimization_barrier((send, anchors[gi - 2]))[0]
        recv = lax.all_to_all(
            send.reshape(n_mem, n_ex, capacity, features + lanes), "expert", split_axis=1, concat_axis=1, tiled=True
        ).reshape(n_mem * block_slots, features + lanes)
        both = lax.all_gather(recv, "tensor")
        routed_x = both[0, :, :features]
        routed_dy = both[1, :, :features]
        routed_gate = both[0, :, features]

        gate_pre = jnp.dot(routed_x, weight_g, preferred_element_type=jnp.float32)
        up_pre = jnp.dot(routed_x, weight_u, preferred_element_type=jnp.float32)
        sig_gate = jax.nn.sigmoid(gate_pre)
        silu_gate = gate_pre * sig_gate
        activation = (silu_gate * up_pre).astype(jnp.bfloat16)
        hidden_grad = lax.dot_general(
            routed_dy, weight_d, (((1,), (1,)), ((), ())), preferred_element_type=jnp.float32
        )
        gate_terms = jnp.sum(hidden_grad * activation.astype(jnp.float32), axis=1)
        row_gate = routed_gate.astype(jnp.float32)[:, None]
        scaled = row_gate * hidden_grad
        up_grad = (scaled * silu_gate).astype(jnp.bfloat16)
        pre_grad = (scaled * up_pre * sig_gate * (1.0 + gate_pre * (1.0 - sig_gate))).astype(
            jnp.bfloat16
        )
        anchors.append(pre_grad)
        weighted = (row_gate * activation.astype(jnp.float32)).astype(jnp.bfloat16)
        rows_x.append(routed_x)
        rows_dy.append(routed_dy)
        rows_pre.append(pre_grad)
        rows_up.append(up_grad)
        rows_w.append(weighted)
        gate_col = jnp.pad(gate_terms[:, None], ((0, 0), (0, lanes - 1)))
        pieces = []
        half = features // 2
        for h in range(2):
            rows = slice(h * half, (h + 1) * half)
            pieces.append(
                lax.dot_general(
                    pre_grad, weight_g[rows], (((1,), (1,)), ((), ())), preferred_element_type=jnp.float32
                ) + lax.dot_general(
                    up_grad, weight_u[rows], (((1,), (1,)), ((), ())), preferred_element_type=jnp.float32
                )
            )
            pieces.append(gate_col)
        ret = lax.psum_scatter(
            jnp.concatenate(pieces, axis=1), "tensor", scatter_dimension=1, tiled=True
        ).astype(jnp.bfloat16)
        back = lax.all_to_all(
            ret.reshape(n_mem, n_ex, capacity, half + lanes), "expert", split_axis=1, concat_axis=1, tiled=True
        ).reshape(n_mem, block_slots, half + lanes)

        for m, s in enumerate(members):
            col_grad = lax.dot_general(
                selects[m], back[m, :, :half], (((0,), (0,)), ((), ())), preferred_element_type=jnp.float32
            )
            col_gate = jnp.sum(
                jnp.where(matches[m], back[m, :, half].astype(jnp.float32)[:, None, None], 0.0), axis=0
            )
            part = jnp.concatenate(
                [col_grad, jnp.pad(col_gate, ((0, 0), (0, lanes - top_count)))], axis=1
            ).astype(jnp.bfloat16)
            if s:
                part = lax.ppermute(part, "dp", [(i, (i - s) % n_dp) for i in range(n_dp)])
            col_parts.append(part.astype(jnp.float32))

    total = sum(col_parts[1:], col_parts[0])
    half = total.shape[1] - lanes
    token_grad = total[:, :half].astype(jnp.bfloat16)
    gate_grad = total[:, half:half + top_count].astype(jnp.bfloat16)
    all_x = jnp.concatenate(rows_x, axis=0)
    all_dy = jnp.concatenate(rows_dy, axis=0)
    grad_g = lax.dot_general(
        all_x, jnp.concatenate(rows_pre, axis=0), (((0,), (0,)), ((), ())),
        preferred_element_type=jnp.float32,
    ).astype(jnp.bfloat16)
    grad_u = lax.dot_general(
        all_x, jnp.concatenate(rows_up, axis=0), (((0,), (0,)), ((), ())),
        preferred_element_type=jnp.float32,
    ).astype(jnp.bfloat16)
    grad_d = lax.dot_general(
        jnp.concatenate(rows_w, axis=0), all_dy, (((0,), (0,)), ((), ())),
        preferred_element_type=jnp.float32,
    ).astype(jnp.bfloat16)
    return (token_grad, gate_grad, grad_g[None], grad_u[None], grad_d[None])


def solution(mesh):
    in_specs = (
        P(("dp", "expert"), None),
        P(("dp", "expert"), None),
        P(("dp", "expert"), None),
        P(("dp", "expert"), None),
        P(("dp", "expert"), None, "tensor"),
        P(("dp", "expert"), None, "tensor"),
        P(("dp", "expert"), "tensor", None),
    )
    out_specs = (
        P(("dp", "expert"), "tensor"),
        P(("dp", "expert"), None),
        P(("dp", "expert"), None, "tensor"),
        P(("dp", "expert"), None, "tensor"),
        P(("dp", "expert"), "tensor", None),
    )
    return jax.shard_map(
        on_device, mesh=mesh, in_specs=in_specs, out_specs=out_specs, check_vma=False
    )
```

```python
import jax
import jax.numpy as jnp
from jax import lax
from jax.sharding import PartitionSpec as P


def on_device(tokens, grad_out, route_ids, gate_values, gate_proj, up_proj, down_proj):
    tok_rows, features = tokens.shape
    top_count = route_ids.shape[1]
    n_dp = lax.axis_size("dp")
    n_ex = lax.axis_size("expert")
    groups = n_dp * n_ex
    capacity = max(2, tok_rows * top_count * 9 // (8 * groups))
    plane = lax.axis_index("dp")
    core = lax.axis_index("tensor")
    routes = tok_rows * top_count
    block_slots = n_ex * capacity
    lanes = 128

    carried = jnp.where(core == 0, tokens, grad_out)
    aux = jnp.concatenate([route_ids.astype(tokens.dtype), gate_values.astype(tokens.dtype)], axis=1)
    aux = jnp.pad(aux, ((0, 0), (0, lanes - aux.shape[1])))
    ext = jnp.concatenate([carried, aux], axis=1)
    blocks = [ext] + [
        lax.ppermute(ext, "dp", [(i, (i + s) % n_dp) for i in range(n_dp)])
        for s in range(1, n_dp)
    ]

    r_iota = jnp.arange(routes, dtype=jnp.int32)
    earlier = (r_iota[None, :] < r_iota[:, None]).astype(jnp.bfloat16)
    e_iota = jnp.arange(n_ex, dtype=jnp.int32)
    q_iota = jnp.arange(block_slots, dtype=jnp.int32)

    weight_g = gate_proj[0]
    weight_u = up_proj[0]
    weight_d = down_proj[0]
    rows_x, rows_dy, rows_pre, rows_up, rows_w = [], [], [], [], []
    col_parts = []
    anchors = []
    groups_of = [[0]] + ([list(range(1, n_dp))] if n_dp > 1 else [])
    for gi, members in enumerate(groups_of):
        sends, selects, matches = [], [], []
        for s in members:
            blk = blocks[s]
            carried_b = blk[:, :features]
            ids_b = blk[:, features:features + top_count].astype(jnp.int32)
            gates_b = blk[:, features + top_count:features + 2 * top_count].astype(jnp.float32)

            local_ex = ids_b.reshape(routes) - plane * n_ex
            in_plane = (local_ex >= 0) & (local_ex < n_ex)
            one_hot = local_ex[:, None] == e_iota[None, :]
            running = jnp.dot(earlier, one_hot.astype(jnp.bfloat16), preferred_element_type=jnp.float32)
            position = jnp.sum(running * one_hot.astype(jnp.float32), axis=1).astype(jnp.int32)
            key = jnp.where(in_plane, local_ex * capacity + position, -1).reshape(tok_rows, top_count)
            match = key[None, :, :] == q_iota[:, None, None]
            select = jnp.sum(match.astype(jnp.bfloat16), axis=2)
            if s == 0:
                send_rows = jnp.concatenate([
                    jnp.dot(select, tokens, preferred_element_type=jnp.float32).astype(tokens.dtype),
                    jnp.dot(select, grad_out, preferred_element_type=jnp.float32).astype(tokens.dtype),
                ], axis=1)
            else:
                send_rows = jnp.dot(select, carried_b, preferred_element_type=jnp.float32).astype(tokens.dtype)
            send_gate = jnp.sum(jnp.where(match, gates_b[None, :, :], 0.0), axis=(1, 2))
            gate_cols = jnp.pad(send_gate.astype(tokens.dtype)[:, None], ((0, 0), (0, lanes - 1)))
            sends.append(jnp.concatenate([send_rows, gate_cols], axis=1))
            selects.append(select)
            matches.append(match)
        send = jnp.stack(sends)
        n_mem = len(members)

        if gi >= 2:
            send = lax.optimization_barrier((send, anchors[gi - 2]))[0]
        width = send.shape[-1]
        recv = lax.all_to_all(
            send.reshape(n_mem, n_ex, capacity, width), "expert", split_axis=1, concat_axis=1, tiled=True
        ).reshape(n_mem * block_slots, width)
        if members == [0]:
            routed_x = recv[:, :features]
            routed_dy = recv[:, features:2 * features]
            routed_gate = recv[:, 2 * features]
        else:
            both = lax.all_gather(recv, "tensor")
            routed_x = both[0, :, :features]
            routed_dy = both[1, :, :features]
            routed_gate = both[0, :, features]

        gate_pre = jnp.dot(routed_x, weight_g, preferred_element_type=jnp.float32)
        up_pre = jnp.dot(routed_x, weight_u, preferred_element_type=jnp.float32)
        sig_gate = jax.nn.sigmoid(gate_pre)
        silu_gate = gate_pre * sig_gate
        activation = (silu_gate * up_pre).astype(jnp.bfloat16)
        hidden_grad = lax.dot_general(
            routed_dy, weight_d, (((1,), (1,)), ((), ())), preferred_element_type=jnp.float32
        )
        gate_terms = jnp.sum(hidden_grad * activation.astype(jnp.float32), axis=1)
        row_gate = routed_gate.astype(jnp.float32)[:, None]
        scaled = row_gate * hidden_grad
        up_grad = (scaled * silu_gate).astype(jnp.bfloat16)
        pre_grad = (scaled * up_pre * sig_gate * (1.0 + gate_pre * (1.0 - sig_gate))).astype(
            jnp.bfloat16
        )
        anchors.append(pre_grad)
        weighted = (row_gate * activation.astype(jnp.float32)).astype(jnp.bfloat16)
        rows_x.append(routed_x)
        rows_dy.append(routed_dy)
        rows_pre.append(pre_grad)
        rows_up.append(up_grad)
        rows_w.append(weighted)
        gate_col = jnp.pad(gate_terms[:, None], ((0, 0), (0, lanes - 1)))
        pieces = []
        half = features // 2
        for h in range(2):
            rows = slice(h * half, (h + 1) * half)
            pieces.append(
                lax.dot_general(
                    pre_grad, weight_g[rows], (((1,), (1,)), ((), ())), preferred_element_type=jnp.float32
                ) + lax.dot_general(
                    up_grad, weight_u[rows], (((1,), (1,)), ((), ())), preferred_element_type=jnp.float32
                )
            )
            pieces.append(gate_col)
        ret = lax.psum_scatter(
            jnp.concatenate(pieces, axis=1), "tensor", scatter_dimension=1, tiled=True
        ).astype(jnp.bfloat16)
        back = lax.all_to_all(
            ret.reshape(n_mem, n_ex, capacity, half + lanes), "expert", split_axis=1, concat_axis=1, tiled=True
        ).reshape(n_mem, block_slots, half + lanes)

        for m, s in enumerate(members):
            col_grad = lax.dot_general(
                selects[m], back[m, :, :half], (((0,), (0,)), ((), ())), preferred_element_type=jnp.float32
            )
            col_gate = jnp.sum(
                jnp.where(matches[m], back[m, :, half].astype(jnp.float32)[:, None, None], 0.0), axis=0
            )
            part = jnp.concatenate(
                [col_grad, jnp.pad(col_gate, ((0, 0), (0, lanes - top_count)))], axis=1
            ).astype(jnp.bfloat16)
            if s:
                part = lax.ppermute(part, "dp", [(i, (i - s) % n_dp) for i in range(n_dp)])
            col_parts.append(part.astype(jnp.float32))

    total = sum(col_parts[1:], col_parts[0])
    half = total.shape[1] - lanes
    token_grad = total[:, :half].astype(jnp.bfloat16)
    gate_grad = total[:, half:half + top_count].astype(jnp.bfloat16)
    all_x = jnp.concatenate(rows_x, axis=0)
    all_dy = jnp.concatenate(rows_dy, axis=0)
    grad_g = lax.dot_general(
        all_x, jnp.concatenate(rows_pre, axis=0), (((0,), (0,)), ((), ())),
        preferred_element_type=jnp.float32,
    ).astype(jnp.bfloat16)
    grad_u = lax.dot_general(
        all_x, jnp.concatenate(rows_up, axis=0), (((0,), (0,)), ((), ())),
        preferred_element_type=jnp.float32,
    ).astype(jnp.bfloat16)
    grad_d = lax.dot_general(
        jnp.concatenate(rows_w, axis=0), all_dy, (((0,), (0,)), ((), ())),
        preferred_element_type=jnp.float32,
    ).astype(jnp.bfloat16)
    return (token_grad, gate_grad, grad_g[None], grad_u[None], grad_d[None])


def solution(mesh):
    in_specs = (
        P(("dp", "expert"), None),
        P(("dp", "expert"), None),
        P(("dp", "expert"), None),
        P(("dp", "expert"), None),
        P(("dp", "expert"), None, "tensor"),
        P(("dp", "expert"), None, "tensor"),
        P(("dp", "expert"), "tensor", None),
    )
    out_specs = (
        P(("dp", "expert"), "tensor"),
        P(("dp", "expert"), None),
        P(("dp", "expert"), None, "tensor"),
        P(("dp", "expert"), None, "tensor"),
        P(("dp", "expert"), "tensor", None),
    )
    return jax.shard_map(
        on_device, mesh=mesh, in_specs=in_specs, out_specs=out_specs, check_vma=False
    )
```

```python
import jax
import jax.numpy as jnp
from jax import lax
from jax.sharding import PartitionSpec as P


def on_device(tokens, grad_out, route_ids, gate_values, gate_proj, up_proj, down_proj):
    tok_rows, features = tokens.shape
    top_count = route_ids.shape[1]
    n_dp = lax.axis_size("dp")
    n_ex = lax.axis_size("expert")
    groups = n_dp * n_ex
    capacity = max(2, tok_rows * top_count * 9 // (8 * groups))
    plane = lax.axis_index("dp")
    core = lax.axis_index("tensor")
    routes = tok_rows * top_count
    block_slots = n_ex * capacity
    lanes = 128

    carried = jnp.where(core == 0, tokens, grad_out)
    aux = jnp.concatenate([route_ids.astype(tokens.dtype), gate_values.astype(tokens.dtype)], axis=1)
    aux = jnp.pad(aux, ((0, 0), (0, lanes - aux.shape[1])))
    ext = jnp.concatenate([carried, aux], axis=1)
    blocks = [ext] + [
        lax.ppermute(ext, "dp", [(i, (i + s) % n_dp) for i in range(n_dp)])
        for s in range(1, n_dp)
    ]

    r_iota = jnp.arange(routes, dtype=jnp.int32)
    earlier = (r_iota[None, :] < r_iota[:, None]).astype(jnp.bfloat16)
    e_iota = jnp.arange(n_ex, dtype=jnp.int32)
    q_iota = jnp.arange(block_slots, dtype=jnp.int32)

    weight_g = gate_proj[0]
    weight_u = up_proj[0]
    weight_d = down_proj[0]
    rows_x, rows_dy, rows_pre, rows_up, rows_w = [], [], [], [], []
    col_parts = []
    anchors = []
    groups_of = [[0]] + ([list(range(1, n_dp))] if n_dp > 1 else [])
    for gi, members in enumerate(groups_of):
        sends, selects, matches = [], [], []
        for s in members:
            blk = blocks[s]
            if gi:
                blk = lax.optimization_barrier((blk, anchors[0]))[0]
            carried_b = blk[:, :features]
            ids_b = blk[:, features:features + top_count].astype(jnp.int32)
            gates_b = blk[:, features + top_count:features + 2 * top_count].astype(jnp.float32)

            local_ex = ids_b.reshape(routes) - plane * n_ex
            in_plane = (local_ex >= 0) & (local_ex < n_ex)
            one_hot = local_ex[:, None] == e_iota[None, :]
            running = jnp.dot(earlier, one_hot.astype(jnp.bfloat16), preferred_element_type=jnp.float32)
            position = jnp.sum(running * one_hot.astype(jnp.float32), axis=1).astype(jnp.int32)
            key = jnp.where(in_plane, local_ex * capacity + position, -1).reshape(tok_rows, top_count)
            match = key[None, :, :] == q_iota[:, None, None]
            select = jnp.sum(match.astype(jnp.bfloat16), axis=2)
            send_rows = jnp.dot(select, carried_b, preferred_element_type=jnp.float32).astype(tokens.dtype)
            send_gate = jnp.sum(jnp.where(match, gates_b[None, :, :], 0.0), axis=(1, 2))
            gate_cols = jnp.pad(send_gate.astype(tokens.dtype)[:, None], ((0, 0), (0, lanes - 1)))
            sends.append(jnp.concatenate([send_rows, gate_cols], axis=1))
            selects.append(select)
            matches.append(match)
        send = jnp.stack(sends)
        n_mem = len(members)

        if gi >= 2:
            send = lax.optimization_barrier((send, anchors[gi - 2]))[0]
        recv = lax.all_to_all(
            send.reshape(n_mem, n_ex, capacity, features + lanes), "expert", split_axis=1, concat_axis=1, tiled=True
        ).reshape(n_mem * block_slots, features + lanes)
        both = lax.all_gather(recv, "tensor")
        routed_x = both[0, :, :features]
        routed_dy = both[1, :, :features]
        routed_gate = both[0, :, features]

        gate_pre = jnp.dot(routed_x, weight_g, preferred_element_type=jnp.float32)
        up_pre = jnp.dot(routed_x, weight_u, preferred_element_type=jnp.float32)
        sig_gate = jax.nn.sigmoid(gate_pre)
        silu_gate = gate_pre * sig_gate
        activation = (silu_gate * up_pre).astype(jnp.bfloat16)
        hidden_grad = lax.dot_general(
            routed_dy, weight_d, (((1,), (1,)), ((), ())), preferred_element_type=jnp.float32
        )
        gate_terms = jnp.sum(hidden_grad * activation.astype(jnp.float32), axis=1)
        row_gate = routed_gate.astype(jnp.float32)[:, None]
        scaled = row_gate * hidden_grad
        up_grad = (scaled * silu_gate).astype(jnp.bfloat16)
        pre_grad = (scaled * up_pre * sig_gate * (1.0 + gate_pre * (1.0 - sig_gate))).astype(
            jnp.bfloat16
        )
        anchors.append(pre_grad)
        weighted = (row_gate * activation.astype(jnp.float32)).astype(jnp.bfloat16)
        rows_x.append(routed_x)
        rows_dy.append(routed_dy)
        rows_pre.append(pre_grad)
        rows_up.append(up_grad)
        rows_w.append(weighted)
        gate_col = jnp.pad(gate_terms[:, None], ((0, 0), (0, lanes - 1)))
        pieces = []
        half = features // 2
        for h in range(2):
            rows = slice(h * half, (h + 1) * half)
            pieces.append(
                lax.dot_general(
                    pre_grad, weight_g[rows], (((1,), (1,)), ((), ())), preferred_element_type=jnp.float32
                ) + lax.dot_general(
                    up_grad, weight_u[rows], (((1,), (1,)), ((), ())), preferred_element_type=jnp.float32
                )
            )
            pieces.append(gate_col)
        ret = lax.psum_scatter(
            jnp.concatenate(pieces, axis=1), "tensor", scatter_dimension=1, tiled=True
        ).astype(jnp.bfloat16)
        back = lax.all_to_all(
            ret.reshape(n_mem, n_ex, capacity, half + lanes), "expert", split_axis=1, concat_axis=1, tiled=True
        ).reshape(n_mem, block_slots, half + lanes)

        for m, s in enumerate(members):
            col_grad = lax.dot_general(
                selects[m], back[m, :, :half], (((0,), (0,)), ((), ())), preferred_element_type=jnp.float32
            )
            col_gate = jnp.sum(
                jnp.where(matches[m], back[m, :, half].astype(jnp.float32)[:, None, None], 0.0), axis=0
            )
            part = jnp.concatenate(
                [col_grad, jnp.pad(col_gate, ((0, 0), (0, lanes - top_count)))], axis=1
            ).astype(jnp.bfloat16)
            if s:
                part = lax.ppermute(part, "dp", [(i, (i - s) % n_dp) for i in range(n_dp)])
            col_parts.append(part.astype(jnp.float32))

    total = sum(col_parts[1:], col_parts[0])
    half = total.shape[1] - lanes
    token_grad = total[:, :half].astype(jnp.bfloat16)
    gate_grad = total[:, half:half + top_count].astype(jnp.bfloat16)
    all_x = jnp.concatenate(rows_x, axis=0)
    all_dy = jnp.concatenate(rows_dy, axis=0)
    grad_g = lax.dot_general(
        all_x, jnp.concatenate(rows_pre, axis=0), (((0,), (0,)), ((), ())),
        preferred_element_type=jnp.float32,
    ).astype(jnp.bfloat16)
    grad_u = lax.dot_general(
        all_x, jnp.concatenate(rows_up, axis=0), (((0,), (0,)), ((), ())),
        preferred_element_type=jnp.float32,
    ).astype(jnp.bfloat16)
    grad_d = lax.dot_general(
        jnp.concatenate(rows_w, axis=0), all_dy, (((0,), (0,)), ((), ())),
        preferred_element_type=jnp.float32,
    ).astype(jnp.bfloat16)
    return (token_grad, gate_grad, grad_g[None], grad_u[None], grad_d[None])


def solution(mesh):
    in_specs = (
        P(("dp", "expert"), None),
        P(("dp", "expert"), None),
        P(("dp", "expert"), None),
        P(("dp", "expert"), None),
        P(("dp", "expert"), None, "tensor"),
        P(("dp", "expert"), None, "tensor"),
        P(("dp", "expert"), "tensor", None),
    )
    out_specs = (
        P(("dp", "expert"), "tensor"),
        P(("dp", "expert"), None),
        P(("dp", "expert"), None, "tensor"),
        P(("dp", "expert"), None, "tensor"),
        P(("dp", "expert"), "tensor", None),
    )
    return jax.shard_map(
        on_device, mesh=mesh, in_specs=in_specs, out_specs=out_specs, check_vma=False
    )
```

```python
import jax
import jax.numpy as jnp
from jax import lax
from jax.sharding import PartitionSpec as P


def on_device(tokens, grad_out, route_ids, gate_values, gate_proj, up_proj, down_proj):
    tok_rows, features = tokens.shape
    top_count = route_ids.shape[1]
    n_dp = lax.axis_size("dp")
    n_ex = lax.axis_size("expert")
    groups = n_dp * n_ex
    capacity = max(2, tok_rows * top_count * 9 // (8 * groups))
    plane = lax.axis_index("dp")
    core = lax.axis_index("tensor")
    routes = tok_rows * top_count
    block_slots = n_ex * capacity
    lanes = 128

    carried = jnp.where(core == 0, tokens, grad_out)
    aux = jnp.concatenate([route_ids.astype(tokens.dtype), gate_values.astype(tokens.dtype)], axis=1)
    aux = jnp.pad(aux, ((0, 0), (0, lanes - aux.shape[1])))
    ext = jnp.concatenate([carried, aux], axis=1)
    blocks = [ext] + [
        lax.ppermute(ext, "dp", [(i, (i + s) % n_dp) for i in range(n_dp)])
        for s in range(1, n_dp)
    ]

    r_iota = jnp.arange(routes, dtype=jnp.int32)
    earlier = (r_iota[None, :] < r_iota[:, None]).astype(jnp.bfloat16)
    e_iota = jnp.arange(n_ex, dtype=jnp.int32)
    q_iota = jnp.arange(block_slots, dtype=jnp.int32)

    weight_g = gate_proj[0]
    weight_u = up_proj[0]
    weight_d = down_proj[0]
    rows_x, rows_dy, rows_pre, rows_up, rows_w = [], [], [], [], []
    col_parts = []
    anchors = []
    groups_of = [[0]] + ([list(range(1, n_dp))] if n_dp > 1 else [])
    for gi, members in enumerate(groups_of):
        n_mem = len(members)
        stacked = jnp.stack([blocks[s] for s in members])
        carried_m = stacked[:, :, :features]
        ids_m = stacked[:, :, features:features + top_count].astype(jnp.int32)
        gates_m = stacked[:, :, features + top_count:features + 2 * top_count].astype(jnp.float32)

        local_ex = ids_m.reshape(n_mem, routes) - plane * n_ex
        in_plane = (local_ex >= 0) & (local_ex < n_ex)
        one_hot = local_ex[:, :, None] == e_iota[None, None, :]
        running = jnp.einsum(
            "ab,mbe->mae", earlier, one_hot.astype(jnp.bfloat16), preferred_element_type=jnp.float32
        )
        position = jnp.sum(running * one_hot.astype(jnp.float32), axis=2).astype(jnp.int32)
        key = jnp.where(in_plane, local_ex * capacity + position, -1).reshape(n_mem, tok_rows, top_count)
        match = key[:, None, :, :] == q_iota[None, :, None, None]
        select = jnp.sum(match.astype(jnp.bfloat16), axis=3)
        send_rows = jnp.einsum(
            "mqt,mtf->mqf", select, carried_m, preferred_element_type=jnp.float32
        ).astype(tokens.dtype)
        send_gate = jnp.sum(jnp.where(match, gates_m[:, None, :, :], 0.0), axis=(2, 3))
        gate_cols = jnp.pad(send_gate.astype(tokens.dtype)[:, :, None], ((0, 0), (0, 0), (0, lanes - 1)))
        send = jnp.concatenate([send_rows, gate_cols], axis=2)

        if gi >= 2:
            send = lax.optimization_barrier((send, anchors[gi - 2]))[0]
        recv = lax.all_to_all(
            send.reshape(n_mem, n_ex, capacity, features + lanes), "expert", split_axis=1, concat_axis=1, tiled=True
        ).reshape(n_mem * block_slots, features + lanes)
        both = lax.all_gather(recv, "tensor")
        routed_x = both[0, :, :features]
        routed_dy = both[1, :, :features]
        routed_gate = both[0, :, features]

        gate_pre = jnp.dot(routed_x, weight_g, preferred_element_type=jnp.float32)
        up_pre = jnp.dot(routed_x, weight_u, preferred_element_type=jnp.float32)
        sig_gate = jax.nn.sigmoid(gate_pre)
        silu_gate = gate_pre * sig_gate
        activation = (silu_gate * up_pre).astype(jnp.bfloat16)
        hidden_grad = lax.dot_general(
            routed_dy, weight_d, (((1,), (1,)), ((), ())), preferred_element_type=jnp.float32
        )
        gate_terms = jnp.sum(hidden_grad * activation.astype(jnp.float32), axis=1)
        row_gate = routed_gate.astype(jnp.float32)[:, None]
        scaled = row_gate * hidden_grad
        up_grad = (scaled * silu_gate).astype(jnp.bfloat16)
        pre_grad = (scaled * up_pre * sig_gate * (1.0 + gate_pre * (1.0 - sig_gate))).astype(
            jnp.bfloat16
        )
        anchors.append(pre_grad)
        weighted = (row_gate * activation.astype(jnp.float32)).astype(jnp.bfloat16)
        rows_x.append(routed_x)
        rows_dy.append(routed_dy)
        rows_pre.append(pre_grad)
        rows_up.append(up_grad)
        rows_w.append(weighted)
        gate_col = jnp.pad(gate_terms[:, None], ((0, 0), (0, lanes - 1)))
        pieces = []
        half = features // 2
        for h in range(2):
            rows = slice(h * half, (h + 1) * half)
            pieces.append(
                lax.dot_general(
                    pre_grad, weight_g[rows], (((1,), (1,)), ((), ())), preferred_element_type=jnp.float32
                ) + lax.dot_general(
                    up_grad, weight_u[rows], (((1,), (1,)), ((), ())), preferred_element_type=jnp.float32
                )
            )
            pieces.append(gate_col)
        ret = lax.psum_scatter(
            jnp.concatenate(pieces, axis=1), "tensor", scatter_dimension=1, tiled=True
        ).astype(jnp.bfloat16)
        back = lax.all_to_all(
            ret.reshape(n_mem, n_ex, capacity, half + lanes), "expert", split_axis=1, concat_axis=1, tiled=True
        ).reshape(n_mem, block_slots, half + lanes)

        col_grad = jnp.einsum(
            "mqt,mqf->mtf", select, back[:, :, :half], preferred_element_type=jnp.float32
        )
        col_gate = jnp.sum(
            jnp.where(match, back[:, :, half].astype(jnp.float32)[:, :, None, None], 0.0), axis=1
        )
        parts = jnp.concatenate(
            [col_grad, jnp.pad(col_gate, ((0, 0), (0, 0), (0, lanes - top_count)))], axis=2
        ).astype(jnp.bfloat16)
        for m, s in enumerate(members):
            part = parts[m]
            if s:
                part = lax.ppermute(part, "dp", [(i, (i - s) % n_dp) for i in range(n_dp)])
            col_parts.append(part.astype(jnp.float32))

    total = sum(col_parts[1:], col_parts[0])
    half = total.shape[1] - lanes
    token_grad = total[:, :half].astype(jnp.bfloat16)
    gate_grad = total[:, half:half + top_count].astype(jnp.bfloat16)
    all_x = jnp.concatenate(rows_x, axis=0)
    all_dy = jnp.concatenate(rows_dy, axis=0)
    grad_g = lax.dot_general(
        all_x, jnp.concatenate(rows_pre, axis=0), (((0,), (0,)), ((), ())),
        preferred_element_type=jnp.float32,
    ).astype(jnp.bfloat16)
    grad_u = lax.dot_general(
        all_x, jnp.concatenate(rows_up, axis=0), (((0,), (0,)), ((), ())),
        preferred_element_type=jnp.float32,
    ).astype(jnp.bfloat16)
    grad_d = lax.dot_general(
        jnp.concatenate(rows_w, axis=0), all_dy, (((0,), (0,)), ((), ())),
        preferred_element_type=jnp.float32,
    ).astype(jnp.bfloat16)
    return (token_grad, gate_grad, grad_g[None], grad_u[None], grad_d[None])


def solution(mesh):
    in_specs = (
        P(("dp", "expert"), None),
        P(("dp", "expert"), None),
        P(("dp", "expert"), None),
        P(("dp", "expert"), None),
        P(("dp", "expert"), None, "tensor"),
        P(("dp", "expert"), None, "tensor"),
        P(("dp", "expert"), "tensor", None),
    )
    out_specs = (
        P(("dp", "expert"), "tensor"),
        P(("dp", "expert"), None),
        P(("dp", "expert"), None, "tensor"),
        P(("dp", "expert"), None, "tensor"),
        P(("dp", "expert"), "tensor", None),
    )
    return jax.shard_map(
        on_device, mesh=mesh, in_specs=in_specs, out_specs=out_specs, check_vma=False
    )
```

```python
import jax
import jax.numpy as jnp
from jax import lax
from jax.sharding import PartitionSpec as P


def on_device(tokens, grad_out, route_ids, gate_values, gate_proj, up_proj, down_proj):
    tok_rows, features = tokens.shape
    top_count = route_ids.shape[1]
    n_dp = lax.axis_size("dp")
    n_ex = lax.axis_size("expert")
    groups = n_dp * n_ex
    capacity = max(2, tok_rows * top_count * 9 // (8 * groups))
    plane = lax.axis_index("dp")
    core = lax.axis_index("tensor")
    routes = tok_rows * top_count
    block_slots = n_ex * capacity
    lanes = 128

    carried = jnp.where(core == 0, tokens, grad_out)
    aux = jnp.concatenate([route_ids.astype(tokens.dtype), gate_values.astype(tokens.dtype)], axis=1)
    aux = jnp.pad(aux, ((0, 0), (0, lanes - aux.shape[1])))
    ext = jnp.concatenate([carried, aux], axis=1)
    blocks = [ext] + [
        lax.ppermute(ext, "dp", [(i, (i + s) % n_dp) for i in range(n_dp)])
        for s in range(1, n_dp)
    ]

    r_iota = jnp.arange(routes, dtype=jnp.int32)
    earlier = (r_iota[None, :] < r_iota[:, None]).astype(jnp.bfloat16)
    e_iota = jnp.arange(n_ex, dtype=jnp.int32)
    q_iota = jnp.arange(block_slots, dtype=jnp.int32)

    weight_g = gate_proj[0]
    weight_u = up_proj[0]
    weight_d = down_proj[0]
    rows_x, rows_dy, rows_pre, rows_up, rows_w = [], [], [], [], []
    col_parts = []
    anchors = []
    groups_of = [[0]] + ([list(range(1, n_dp))] if n_dp > 1 else [])
    for gi, members in enumerate(groups_of):
        n_mem = len(members)
        stacked = jnp.stack([blocks[s] for s in members])
        carried_m = stacked[:, :, :features]
        ids_m = stacked[:, :, features:features + top_count].astype(jnp.int32)
        gates_m = stacked[:, :, features + top_count:features + 2 * top_count].astype(jnp.float32)

        local_ex = ids_m.reshape(n_mem, routes) - plane * n_ex
        in_plane = (local_ex >= 0) & (local_ex < n_ex)
        one_hot = local_ex[:, :, None] == e_iota[None, None, :]
        running = jnp.einsum(
            "ab,mbe->mae", earlier, one_hot.astype(jnp.bfloat16), preferred_element_type=jnp.float32
        )
        position = jnp.sum(running * one_hot.astype(jnp.float32), axis=2).astype(jnp.int32)
        key = jnp.where(in_plane, local_ex * capacity + position, -1).reshape(n_mem, tok_rows, top_count)
        match = key[:, None, :, :] == q_iota[None, :, None, None]
        select = jnp.sum(match.astype(jnp.bfloat16), axis=3)
        send_rows = jnp.einsum(
            "mqt,mtf->mqf", select, carried_m, preferred_element_type=jnp.float32
        ).astype(tokens.dtype)
        send_gate = jnp.sum(jnp.where(match, gates_m[:, None, :, :], 0.0), axis=(2, 3))
        gate_cols = jnp.pad(send_gate.astype(tokens.dtype)[:, :, None], ((0, 0), (0, 0), (0, lanes - 1)))
        send = jnp.concatenate([send_rows, gate_cols], axis=2)

        if gi >= 2:
            send = lax.optimization_barrier((send, anchors[gi - 2]))[0]
        recv = lax.all_to_all(
            send.reshape(n_mem, n_ex, capacity, features + lanes), "expert", split_axis=1, concat_axis=1, tiled=True
        ).reshape(n_mem * block_slots, features + lanes)
        other = lax.ppermute(recv, "tensor", [(0, 1), (1, 0)])
        mine_x = core == 0
        routed_x = jnp.where(mine_x, recv[:, :features], other[:, :features])
        routed_dy = jnp.where(mine_x, other[:, :features], recv[:, :features])
        routed_gate = jnp.where(mine_x, recv[:, features], other[:, features])

        gate_pre = jnp.dot(routed_x, weight_g, preferred_element_type=jnp.float32)
        up_pre = jnp.dot(routed_x, weight_u, preferred_element_type=jnp.float32)
        sig_gate = jax.nn.sigmoid(gate_pre)
        silu_gate = gate_pre * sig_gate
        activation = (silu_gate * up_pre).astype(jnp.bfloat16)
        hidden_grad = lax.dot_general(
            routed_dy, weight_d, (((1,), (1,)), ((), ())), preferred_element_type=jnp.float32
        )
        gate_terms = jnp.sum(hidden_grad * activation.astype(jnp.float32), axis=1)
        row_gate = routed_gate.astype(jnp.float32)[:, None]
        scaled = row_gate * hidden_grad
        up_grad = (scaled * silu_gate).astype(jnp.bfloat16)
        pre_grad = (scaled * up_pre * sig_gate * (1.0 + gate_pre * (1.0 - sig_gate))).astype(
            jnp.bfloat16
        )
        anchors.append(pre_grad)
        weighted = (row_gate * activation.astype(jnp.float32)).astype(jnp.bfloat16)
        rows_x.append(routed_x)
        rows_dy.append(routed_dy)
        rows_pre.append(pre_grad)
        rows_up.append(up_grad)
        rows_w.append(weighted)
        gate_col = jnp.pad(gate_terms[:, None], ((0, 0), (0, lanes - 1)))
        pieces = []
        half = features // 2
        for h in range(2):
            rows = slice(h * half, (h + 1) * half)
            pieces.append(
                lax.dot_general(
                    pre_grad, weight_g[rows], (((1,), (1,)), ((), ())), preferred_element_type=jnp.float32
                ) + lax.dot_general(
                    up_grad, weight_u[rows], (((1,), (1,)), ((), ())), preferred_element_type=jnp.float32
                )
            )
            pieces.append(gate_col)
        ret = lax.psum_scatter(
            jnp.concatenate(pieces, axis=1), "tensor", scatter_dimension=1, tiled=True
        ).astype(jnp.bfloat16)
        back = lax.all_to_all(
            ret.reshape(n_mem, n_ex, capacity, half + lanes), "expert", split_axis=1, concat_axis=1, tiled=True
        ).reshape(n_mem, block_slots, half + lanes)

        col_grad = jnp.einsum(
            "mqt,mqf->mtf", select, back[:, :, :half], preferred_element_type=jnp.float32
        )
        col_gate = jnp.sum(
            jnp.where(match, back[:, :, half].astype(jnp.float32)[:, :, None, None], 0.0), axis=1
        )
        parts = jnp.concatenate(
            [col_grad, jnp.pad(col_gate, ((0, 0), (0, 0), (0, lanes - top_count)))], axis=2
        ).astype(jnp.bfloat16)
        for m, s in enumerate(members):
            part = parts[m]
            if s:
                part = lax.ppermute(part, "dp", [(i, (i - s) % n_dp) for i in range(n_dp)])
            col_parts.append(part.astype(jnp.float32))

    total = sum(col_parts[1:], col_parts[0])
    half = total.shape[1] - lanes
    token_grad = total[:, :half].astype(jnp.bfloat16)
    gate_grad = total[:, half:half + top_count].astype(jnp.bfloat16)
    all_x = jnp.concatenate(rows_x, axis=0)
    all_dy = jnp.concatenate(rows_dy, axis=0)
    grad_g = lax.dot_general(
        all_x, jnp.concatenate(rows_pre, axis=0), (((0,), (0,)), ((), ())),
        preferred_element_type=jnp.float32,
    ).astype(jnp.bfloat16)
    grad_u = lax.dot_general(
        all_x, jnp.concatenate(rows_up, axis=0), (((0,), (0,)), ((), ())),
        preferred_element_type=jnp.float32,
    ).astype(jnp.bfloat16)
    grad_d = lax.dot_general(
        jnp.concatenate(rows_w, axis=0), all_dy, (((0,), (0,)), ((), ())),
        preferred_element_type=jnp.float32,
    ).astype(jnp.bfloat16)
    return (token_grad, gate_grad, grad_g[None], grad_u[None], grad_d[None])


def solution(mesh):
    in_specs = (
        P(("dp", "expert"), None),
        P(("dp", "expert"), None),
        P(("dp", "expert"), None),
        P(("dp", "expert"), None),
        P(("dp", "expert"), None, "tensor"),
        P(("dp", "expert"), None, "tensor"),
        P(("dp", "expert"), "tensor", None),
    )
    out_specs = (
        P(("dp", "expert"), "tensor"),
        P(("dp", "expert"), None),
        P(("dp", "expert"), None, "tensor"),
        P(("dp", "expert"), None, "tensor"),
        P(("dp", "expert"), "tensor", None),
    )
    return jax.shard_map(
        on_device, mesh=mesh, in_specs=in_specs, out_specs=out_specs, check_vma=False
    )
```

```python
import jax
import jax.numpy as jnp
from jax import lax
from jax.sharding import PartitionSpec as P


def on_device(tokens, grad_out, route_ids, gate_values, gate_proj, up_proj, down_proj):
    tok_rows, features = tokens.shape
    top_count = route_ids.shape[1]
    n_dp = lax.axis_size("dp")
    n_ex = lax.axis_size("expert")
    groups = n_dp * n_ex
    capacity = max(2, tok_rows * top_count * 9 // (8 * groups))
    plane = lax.axis_index("dp")
    core = lax.axis_index("tensor")
    routes = tok_rows * top_count
    block_slots = n_ex * capacity
    lanes = 128

    carried = jnp.where(core == 0, tokens, grad_out)
    aux = jnp.concatenate([route_ids.astype(tokens.dtype), gate_values.astype(tokens.dtype)], axis=1)
    aux = jnp.pad(aux, ((0, 0), (0, lanes - aux.shape[1])))
    ext = jnp.concatenate([carried, aux], axis=1)
    blocks = [ext] + [
        lax.ppermute(ext, "dp", [(i, (i + s) % n_dp) for i in range(n_dp)])
        for s in range(1, n_dp)
    ]

    r_iota = jnp.arange(routes, dtype=jnp.int32)
    earlier = (r_iota[None, :] < r_iota[:, None]).astype(jnp.bfloat16)
    e_iota = jnp.arange(n_ex, dtype=jnp.int32)
    q_iota = jnp.arange(block_slots, dtype=jnp.int32)

    weight_g = gate_proj[0]
    weight_u = up_proj[0]
    weight_d = down_proj[0]
    rows_x, rows_dy, rows_pre, rows_up, rows_w = [], [], [], [], []
    col_parts = []
    anchors = []
    groups_of = [[0]] + ([list(range(1, n_dp))] if n_dp > 1 else [])
    for gi, members in enumerate(groups_of):
        n_mem = len(members)
        stacked = jnp.stack([blocks[s] for s in members])
        carried_m = stacked[:, :, :features]
        ids_m = stacked[:, :, features:features + top_count].astype(jnp.int32)
        gates_m = stacked[:, :, features + top_count:features + 2 * top_count].astype(jnp.float32)

        local_ex = ids_m.reshape(n_mem, routes) - plane * n_ex
        in_plane = (local_ex >= 0) & (local_ex < n_ex)
        one_hot = local_ex[:, :, None] == e_iota[None, None, :]
        running = jnp.einsum(
            "ab,mbe->mae", earlier, one_hot.astype(jnp.bfloat16), preferred_element_type=jnp.float32
        )
        position = jnp.sum(running * one_hot.astype(jnp.float32), axis=2).astype(jnp.int32)
        key = jnp.where(in_plane, local_ex * capacity + position, -1).reshape(n_mem, tok_rows, top_count)
        match = key[:, None, :, :] == q_iota[None, :, None, None]
        select = jnp.sum(match.astype(jnp.bfloat16), axis=3)
        send_rows = jnp.einsum(
            "mqt,mtf->mqf", select, carried_m, preferred_element_type=jnp.float32
        ).astype(tokens.dtype)
        send_gate = jnp.sum(jnp.where(match, gates_m[:, None, :, :], 0.0), axis=(2, 3))
        gate_cols = jnp.pad(send_gate.astype(tokens.dtype)[:, :, None], ((0, 0), (0, 0), (0, lanes - 1)))
        send = jnp.concatenate([send_rows, gate_cols], axis=2)

        if gi >= 2:
            send = lax.optimization_barrier((send, anchors[gi - 2]))[0]
        recv = lax.all_to_all(
            send.reshape(n_mem, n_ex, capacity, features + lanes), "expert", split_axis=1, concat_axis=1, tiled=True
        ).reshape(n_mem * block_slots, features + lanes)
        other = lax.ppermute(recv, "tensor", [(0, 1), (1, 0)])
        mine_x = core == 0
        routed_x = jnp.where(mine_x, recv[:, :features], other[:, :features])
        routed_dy = jnp.where(mine_x, other[:, :features], recv[:, :features])
        routed_gate = jnp.where(mine_x, recv[:, features], other[:, features])

        gate_pre = jnp.dot(routed_x, weight_g, preferred_element_type=jnp.float32)
        up_pre = jnp.dot(routed_x, weight_u, preferred_element_type=jnp.float32)
        sig_gate = jax.nn.sigmoid(gate_pre)
        silu_gate = gate_pre * sig_gate
        activation = (silu_gate * up_pre).astype(jnp.bfloat16)
        hidden_grad = lax.dot_general(
            routed_dy, weight_d, (((1,), (1,)), ((), ())), preferred_element_type=jnp.float32
        )
        gate_terms = jnp.sum(hidden_grad * activation.astype(jnp.float32), axis=1)
        row_gate = routed_gate.astype(jnp.float32)[:, None]
        scaled = row_gate * hidden_grad
        up_grad = (scaled * silu_gate).astype(jnp.bfloat16)
        pre_grad = (scaled * up_pre * sig_gate * (1.0 + gate_pre * (1.0 - sig_gate))).astype(
            jnp.bfloat16
        )
        anchors.append(pre_grad)
        weighted = (row_gate * activation.astype(jnp.float32)).astype(jnp.bfloat16)
        rows_x.append(routed_x)
        rows_dy.append(routed_dy)
        rows_pre.append(pre_grad)
        rows_up.append(up_grad)
        rows_w.append(weighted)
        gate_col = jnp.pad(gate_terms[:, None], ((0, 0), (0, lanes - 1)))
        half = features // 2

        def hidden_part(c):
            w_g = lax.dynamic_slice_in_dim(weight_g, c * half, half, axis=0)
            w_u = lax.dynamic_slice_in_dim(weight_u, c * half, half, axis=0)
            return jnp.concatenate([
                lax.dot_general(
                    pre_grad, w_g, (((1,), (1,)), ((), ())), preferred_element_type=jnp.float32
                ) + lax.dot_general(
                    up_grad, w_u, (((1,), (1,)), ((), ())), preferred_element_type=jnp.float32
                ),
                gate_col,
            ], axis=1)

        theirs = lax.ppermute(hidden_part(1 - core), "tensor", [(0, 1), (1, 0)])
        ret = (hidden_part(core) + theirs).astype(jnp.bfloat16)
        back = lax.all_to_all(
            ret.reshape(n_mem, n_ex, capacity, half + lanes), "expert", split_axis=1, concat_axis=1, tiled=True
        ).reshape(n_mem, block_slots, half + lanes)

        col_grad = jnp.einsum(
            "mqt,mqf->mtf", select, back[:, :, :half], preferred_element_type=jnp.float32
        )
        col_gate = jnp.sum(
            jnp.where(match, back[:, :, half].astype(jnp.float32)[:, :, None, None], 0.0), axis=1
        )
        parts = jnp.concatenate(
            [col_grad, jnp.pad(col_gate, ((0, 0), (0, 0), (0, lanes - top_count)))], axis=2
        ).astype(jnp.bfloat16)
        for m, s in enumerate(members):
            part = parts[m]
            if s:
                part = lax.ppermute(part, "dp", [(i, (i - s) % n_dp) for i in range(n_dp)])
            col_parts.append(part.astype(jnp.float32))

    total = sum(col_parts[1:], col_parts[0])
    half = total.shape[1] - lanes
    token_grad = total[:, :half].astype(jnp.bfloat16)
    gate_grad = total[:, half:half + top_count].astype(jnp.bfloat16)
    all_x = jnp.concatenate(rows_x, axis=0)
    all_dy = jnp.concatenate(rows_dy, axis=0)
    grad_g = lax.dot_general(
        all_x, jnp.concatenate(rows_pre, axis=0), (((0,), (0,)), ((), ())),
        preferred_element_type=jnp.float32,
    ).astype(jnp.bfloat16)
    grad_u = lax.dot_general(
        all_x, jnp.concatenate(rows_up, axis=0), (((0,), (0,)), ((), ())),
        preferred_element_type=jnp.float32,
    ).astype(jnp.bfloat16)
    grad_d = lax.dot_general(
        jnp.concatenate(rows_w, axis=0), all_dy, (((0,), (0,)), ((), ())),
        preferred_element_type=jnp.float32,
    ).astype(jnp.bfloat16)
    return (token_grad, gate_grad, grad_g[None], grad_u[None], grad_d[None])


def solution(mesh):
    in_specs = (
        P(("dp", "expert"), None),
        P(("dp", "expert"), None),
        P(("dp", "expert"), None),
        P(("dp", "expert"), None),
        P(("dp", "expert"), None, "tensor"),
        P(("dp", "expert"), None, "tensor"),
        P(("dp", "expert"), "tensor", None),
    )
    out_specs = (
        P(("dp", "expert"), "tensor"),
        P(("dp", "expert"), None),
        P(("dp", "expert"), None, "tensor"),
        P(("dp", "expert"), None, "tensor"),
        P(("dp", "expert"), "tensor", None),
    )
    return jax.shard_map(
        on_device, mesh=mesh, in_specs=in_specs, out_specs=out_specs, check_vma=False
    )
```

```python
import jax
import jax.numpy as jnp
from jax import lax
from jax.sharding import PartitionSpec as P


def on_device(tokens, grad_out, route_ids, gate_values, gate_proj, up_proj, down_proj):
    tok_rows, features = tokens.shape
    top_count = route_ids.shape[1]
    n_dp = lax.axis_size("dp")
    n_ex = lax.axis_size("expert")
    groups = n_dp * n_ex
    capacity = max(2, tok_rows * top_count * 9 // (8 * groups))
    plane = lax.axis_index("dp")
    core = lax.axis_index("tensor")
    routes = tok_rows * top_count
    block_slots = n_ex * capacity
    lanes = 128

    carried = jnp.where(core == 0, tokens, grad_out)
    aux = jnp.concatenate([route_ids.astype(tokens.dtype), gate_values.astype(tokens.dtype)], axis=1)
    aux = jnp.pad(aux, ((0, 0), (0, lanes - aux.shape[1])))
    ext = jnp.concatenate([carried, aux], axis=1)
    blocks = [ext] + [
        lax.ppermute(ext, "dp", [(i, (i + s) % n_dp) for i in range(n_dp)])
        for s in range(1, n_dp)
    ]

    r_iota = jnp.arange(routes, dtype=jnp.int32)
    earlier = (r_iota[None, :] < r_iota[:, None]).astype(jnp.bfloat16)
    e_iota = jnp.arange(n_ex, dtype=jnp.int32)
    q_iota = jnp.arange(block_slots, dtype=jnp.int32)

    weight_g = gate_proj[0]
    weight_u = up_proj[0]
    weight_d = down_proj[0]
    rows_x, rows_dy, rows_pre, rows_up, rows_w = [], [], [], [], []
    col_parts = []
    anchors = []
    groups_of = [[0]] + ([list(range(1, n_dp))] if n_dp > 1 else [])
    for gi, members in enumerate(groups_of):
        n_mem = len(members)
        stacked = jnp.stack([blocks[s] for s in members])
        carried_m = stacked[:, :, :features]
        ids_m = stacked[:, :, features:features + top_count].astype(jnp.int32)
        gates_m = stacked[:, :, features + top_count:features + 2 * top_count].astype(jnp.float32)

        local_ex = ids_m.reshape(n_mem, routes) - plane * n_ex
        in_plane = (local_ex >= 0) & (local_ex < n_ex)
        one_hot = local_ex[:, :, None] == e_iota[None, None, :]
        running = jnp.einsum(
            "ab,mbe->mae", earlier, one_hot.astype(jnp.bfloat16), preferred_element_type=jnp.float32
        )
        position = jnp.sum(running * one_hot.astype(jnp.float32), axis=2).astype(jnp.int32)
        key = jnp.where(in_plane, local_ex * capacity + position, -1).reshape(n_mem, tok_rows, top_count)
        match = key[:, None, :, :] == q_iota[None, :, None, None]
        select = jnp.sum(match.astype(jnp.bfloat16), axis=3)
        send_rows = jnp.einsum(
            "mqt,mtf->mqf", select, carried_m, preferred_element_type=jnp.float32
        ).astype(tokens.dtype)
        send_gate = jnp.sum(jnp.where(match, gates_m[:, None, :, :], 0.0), axis=(2, 3))
        gate_cols = jnp.pad(send_gate.astype(tokens.dtype)[:, :, None], ((0, 0), (0, 0), (0, lanes - 1)))
        send = jnp.concatenate([send_rows, gate_cols], axis=2)

        if gi >= 2:
            send = lax.optimization_barrier((send, anchors[gi - 2]))[0]
        recv = lax.all_to_all(
            send.reshape(n_mem, n_ex, capacity, features + lanes), "expert", split_axis=1, concat_axis=1, tiled=True
        ).reshape(n_mem * block_slots, features + lanes)
        other = lax.ppermute(recv, "tensor", [(0, 1), (1, 0)])
        mine_x = core == 0
        routed_x = jnp.where(mine_x, recv[:, :features], other[:, :features])
        routed_dy = jnp.where(mine_x, other[:, :features], recv[:, :features])
        routed_gate = jnp.where(mine_x, recv[:, features], other[:, features])

        gate_pre = jnp.dot(routed_x, weight_g, preferred_element_type=jnp.float32)
        up_pre = jnp.dot(routed_x, weight_u, preferred_element_type=jnp.float32)
        sig_gate = jax.nn.sigmoid(gate_pre)
        silu_gate = gate_pre * sig_gate
        activation = (silu_gate * up_pre).astype(jnp.bfloat16)
        hidden_grad = lax.dot_general(
            routed_dy, weight_d, (((1,), (1,)), ((), ())), preferred_element_type=jnp.float32
        )
        gate_terms = jnp.sum(hidden_grad * activation.astype(jnp.float32), axis=1)
        row_gate = routed_gate.astype(jnp.float32)[:, None]
        scaled = row_gate * hidden_grad
        up_grad = (scaled * silu_gate).astype(jnp.bfloat16)
        pre_grad = (scaled * up_pre * sig_gate * (1.0 + gate_pre * (1.0 - sig_gate))).astype(
            jnp.bfloat16
        )
        anchors.append(pre_grad)
        weighted = (row_gate * activation.astype(jnp.float32)).astype(jnp.bfloat16)
        rows_x.append(routed_x)
        rows_dy.append(routed_dy)
        rows_pre.append(pre_grad)
        rows_up.append(up_grad)
        rows_w.append(weighted)
        half = features // 2
        partial_value = lax.dot_general(
            pre_grad, weight_g, (((1,), (1,)), ((), ())), preferred_element_type=jnp.float32
        ) + lax.dot_general(
            up_grad, weight_u, (((1,), (1,)), ((), ())), preferred_element_type=jnp.float32
        )
        routed_grad = lax.psum_scatter(
            partial_value.astype(jnp.bfloat16), "tensor", scatter_dimension=1, tiled=True
        )
        slot_gate = lax.psum(gate_terms, "tensor").astype(jnp.bfloat16)
        ret = jnp.concatenate(
            [routed_grad, jnp.pad(slot_gate[:, None], ((0, 0), (0, lanes - 1)))], axis=1
        )
        back = lax.all_to_all(
            ret.reshape(n_mem, n_ex, capacity, half + lanes), "expert", split_axis=1, concat_axis=1, tiled=True
        ).reshape(n_mem, block_slots, half + lanes)

        col_grad = jnp.einsum(
            "mqt,mqf->mtf", select, back[:, :, :half], preferred_element_type=jnp.float32
        )
        col_gate = jnp.sum(
            jnp.where(match, back[:, :, half].astype(jnp.float32)[:, :, None, None], 0.0), axis=1
        )
        parts = jnp.concatenate(
            [col_grad, jnp.pad(col_gate, ((0, 0), (0, 0), (0, lanes - top_count)))], axis=2
        ).astype(jnp.bfloat16)
        for m, s in enumerate(members):
            part = parts[m]
            if s:
                part = lax.ppermute(part, "dp", [(i, (i - s) % n_dp) for i in range(n_dp)])
            col_parts.append(part.astype(jnp.float32))

    total = sum(col_parts[1:], col_parts[0])
    half = total.shape[1] - lanes
    token_grad = total[:, :half].astype(jnp.bfloat16)
    gate_grad = total[:, half:half + top_count].astype(jnp.bfloat16)
    all_x = jnp.concatenate(rows_x, axis=0)
    all_dy = jnp.concatenate(rows_dy, axis=0)
    grad_g = lax.dot_general(
        all_x, jnp.concatenate(rows_pre, axis=0), (((0,), (0,)), ((), ())),
        preferred_element_type=jnp.float32,
    ).astype(jnp.bfloat16)
    grad_u = lax.dot_general(
        all_x, jnp.concatenate(rows_up, axis=0), (((0,), (0,)), ((), ())),
        preferred_element_type=jnp.float32,
    ).astype(jnp.bfloat16)
    grad_d = lax.dot_general(
        jnp.concatenate(rows_w, axis=0), all_dy, (((0,), (0,)), ((), ())),
        preferred_element_type=jnp.float32,
    ).astype(jnp.bfloat16)
    return (token_grad, gate_grad, grad_g[None], grad_u[None], grad_d[None])


def solution(mesh):
    in_specs = (
        P(("dp", "expert"), None),
        P(("dp", "expert"), None),
        P(("dp", "expert"), None),
        P(("dp", "expert"), None),
        P(("dp", "expert"), None, "tensor"),
        P(("dp", "expert"), None, "tensor"),
        P(("dp", "expert"), "tensor", None),
    )
    out_specs = (
        P(("dp", "expert"), "tensor"),
        P(("dp", "expert"), None),
        P(("dp", "expert"), None, "tensor"),
        P(("dp", "expert"), None, "tensor"),
        P(("dp", "expert"), "tensor", None),
    )
    return jax.shard_map(
        on_device, mesh=mesh, in_specs=in_specs, out_specs=out_specs, check_vma=False
    )
```

```python
import jax
import jax.numpy as jnp
from jax import lax
from jax.sharding import PartitionSpec as P


def on_device(tokens, grad_out, route_ids, gate_values, gate_proj, up_proj, down_proj):
    tok_rows, features = tokens.shape
    top_count = route_ids.shape[1]
    n_dp = lax.axis_size("dp")
    n_ex = lax.axis_size("expert")
    groups = n_dp * n_ex
    capacity = max(2, tok_rows * top_count * 9 // (8 * groups))
    plane = lax.axis_index("dp")
    core = lax.axis_index("tensor")
    routes = tok_rows * top_count
    block_slots = n_ex * capacity
    lanes = 128

    carried = jnp.where(core == 0, tokens, grad_out)
    aux = jnp.concatenate([route_ids.astype(tokens.dtype), gate_values.astype(tokens.dtype)], axis=1)
    aux = jnp.pad(aux, ((0, 0), (0, lanes - aux.shape[1])))
    ext = jnp.concatenate([carried, aux], axis=1)
    blocks = [ext] + [
        lax.ppermute(ext, "dp", [(i, (i + s) % n_dp) for i in range(n_dp)])
        for s in range(1, n_dp)
    ]

    r_iota = jnp.arange(routes, dtype=jnp.int32)
    earlier = (r_iota[None, :] < r_iota[:, None]).astype(jnp.bfloat16)
    e_iota = jnp.arange(n_ex, dtype=jnp.int32)
    q_iota = jnp.arange(block_slots, dtype=jnp.int32)

    weight_g = gate_proj[0]
    weight_u = up_proj[0]
    weight_d = down_proj[0]
    rows_x, rows_dy, rows_pre, rows_up, rows_w = [], [], [], [], []
    col_parts = []
    anchors = []
    groups_of = [[0]] + ([list(range(1, n_dp))] if n_dp > 1 else [])
    for gi, members in enumerate(groups_of):
        n_mem = len(members)
        stacked = jnp.stack([blocks[s] for s in members])
        carried_m = stacked[:, :, :features]
        ids_m = stacked[:, :, features:features + top_count].astype(jnp.int32)
        gates_m = stacked[:, :, features + top_count:features + 2 * top_count].astype(jnp.float32)

        local_ex = ids_m.reshape(n_mem, routes) - plane * n_ex
        in_plane = (local_ex >= 0) & (local_ex < n_ex)
        one_hot = local_ex[:, :, None] == e_iota[None, None, :]
        running = jnp.einsum(
            "ab,mbe->mae", earlier, one_hot.astype(jnp.bfloat16), preferred_element_type=jnp.float32
        )
        position = jnp.sum(running * one_hot.astype(jnp.float32), axis=2).astype(jnp.int32)
        key = jnp.where(in_plane, local_ex * capacity + position, -1).reshape(n_mem, tok_rows, top_count)
        match = key[:, None, :, :] == q_iota[None, :, None, None]
        select = jnp.sum(match.astype(jnp.bfloat16), axis=3)
        send_rows = jnp.einsum(
            "mqt,mtf->mqf", select, carried_m, preferred_element_type=jnp.float32
        ).astype(tokens.dtype)
        send_gate = jnp.sum(jnp.where(match, gates_m[:, None, :, :], 0.0), axis=(2, 3))
        gate_cols = jnp.pad(send_gate.astype(tokens.dtype)[:, :, None], ((0, 0), (0, 0), (0, lanes - 1)))
        send = jnp.concatenate([send_rows, gate_cols], axis=2)

        if gi >= 2:
            send = lax.optimization_barrier((send, anchors[gi - 2]))[0]
        recv = lax.all_to_all(
            send.reshape(n_mem, n_ex, capacity, features + lanes), "expert", split_axis=1, concat_axis=1, tiled=True
        ).reshape(n_mem * block_slots, features + lanes)
        other = lax.ppermute(recv, "tensor", [(0, 1), (1, 0)])
        mine_x = core == 0
        routed_x = jnp.where(mine_x, recv[:, :features], other[:, :features])
        routed_dy = jnp.where(mine_x, other[:, :features], recv[:, :features])
        routed_gate = jnp.where(mine_x, recv[:, features], other[:, features])

        gate_pre = jnp.dot(routed_x, weight_g, preferred_element_type=jnp.float32)
        up_pre = jnp.dot(routed_x, weight_u, preferred_element_type=jnp.float32)
        sig_gate = jax.nn.sigmoid(gate_pre)
        silu_gate = gate_pre * sig_gate
        activation = (silu_gate * up_pre).astype(jnp.bfloat16)
        hidden_grad = lax.dot_general(
            routed_dy, weight_d, (((1,), (1,)), ((), ())), preferred_element_type=jnp.float32
        )
        gate_terms = jnp.sum(hidden_grad * activation.astype(jnp.float32), axis=1)
        row_gate = routed_gate.astype(jnp.float32)[:, None]
        scaled = row_gate * hidden_grad
        up_grad = (scaled * silu_gate).astype(jnp.bfloat16)
        pre_grad = (scaled * up_pre * sig_gate * (1.0 + gate_pre * (1.0 - sig_gate))).astype(
            jnp.bfloat16
        )
        anchors.append(pre_grad)
        weighted = (row_gate * activation.astype(jnp.float32)).astype(jnp.bfloat16)
        rows_x.append(routed_x)
        rows_dy.append(routed_dy)
        rows_pre.append(pre_grad)
        rows_up.append(up_grad)
        rows_w.append(weighted)
        gate_col = jnp.pad(gate_terms[:, None], ((0, 0), (0, lanes - 1)))
        pieces = []
        half = features // 2
        for h in range(2):
            rows = slice(h * half, (h + 1) * half)
            pieces.append(
                lax.dot_general(
                    pre_grad, weight_g[rows], (((1,), (1,)), ((), ())), preferred_element_type=jnp.float32
                ) + lax.dot_general(
                    up_grad, weight_u[rows], (((1,), (1,)), ((), ())), preferred_element_type=jnp.float32
                )
            )
            pieces.append(gate_col)
        ret = lax.psum_scatter(
            jnp.concatenate(pieces, axis=1), "tensor", scatter_dimension=1, tiled=True
        ).astype(jnp.bfloat16)
        back = lax.all_to_all(
            ret.reshape(n_mem, n_ex, capacity, half + lanes), "expert", split_axis=1, concat_axis=1, tiled=True
        ).reshape(n_mem, block_slots, half + lanes)

        col_grad = jnp.einsum(
            "mqt,mqf->mtf", select, back[:, :, :half], preferred_element_type=jnp.float32
        )
        col_gate = jnp.sum(
            jnp.where(match, back[:, :, half].astype(jnp.float32)[:, :, None, None], 0.0), axis=1
        )
        parts = jnp.concatenate(
            [col_grad, jnp.pad(col_gate, ((0, 0), (0, 0), (0, lanes - top_count)))], axis=2
        ).astype(jnp.bfloat16)
        for m, s in enumerate(members):
            part = parts[m]
            if s:
                part = lax.ppermute(part, "dp", [(i, (i - s) % n_dp) for i in range(n_dp)])
            col_parts.append(part.astype(jnp.float32))

    total = sum(col_parts[1:], col_parts[0])
    half = total.shape[1] - lanes
    token_grad = total[:, :half].astype(jnp.bfloat16)
    gate_grad = total[:, half:half + top_count].astype(jnp.bfloat16)
    def over_groups(lhs, rhs):
        total_w = None
        for l, r in zip(lhs, rhs):
            term = lax.dot_general(l, r, (((0,), (0,)), ((), ())), preferred_element_type=jnp.float32)
            total_w = term if total_w is None else total_w + term
        return total_w.astype(jnp.bfloat16)

    grad_g = over_groups(rows_x, rows_pre)
    grad_u = over_groups(rows_x, rows_up)
    grad_d = over_groups(rows_w, rows_dy)
    return (token_grad, gate_grad, grad_g[None], grad_u[None], grad_d[None])


def solution(mesh):
    in_specs = (
        P(("dp", "expert"), None),
        P(("dp", "expert"), None),
        P(("dp", "expert"), None),
        P(("dp", "expert"), None),
        P(("dp", "expert"), None, "tensor"),
        P(("dp", "expert"), None, "tensor"),
        P(("dp", "expert"), "tensor", None),
    )
    out_specs = (
        P(("dp", "expert"), "tensor"),
        P(("dp", "expert"), None),
        P(("dp", "expert"), None, "tensor"),
        P(("dp", "expert"), None, "tensor"),
        P(("dp", "expert"), "tensor", None),
    )
    return jax.shard_map(
        on_device, mesh=mesh, in_specs=in_specs, out_specs=out_specs, check_vma=False
    )
```

```python
import jax
import jax.numpy as jnp
from jax import lax
from jax.sharding import PartitionSpec as P


def on_device(tokens, grad_out, route_ids, gate_values, gate_proj, up_proj, down_proj):
    tok_rows, features = tokens.shape
    top_count = route_ids.shape[1]
    n_dp = lax.axis_size("dp")
    n_ex = lax.axis_size("expert")
    groups = n_dp * n_ex
    capacity = max(2, tok_rows * top_count * 9 // (8 * groups))
    plane = lax.axis_index("dp")
    core = lax.axis_index("tensor")
    routes = tok_rows * top_count
    block_slots = n_ex * capacity
    lanes = 128

    carried = jnp.where(core == 0, tokens, grad_out)
    aux = jnp.concatenate([route_ids.astype(tokens.dtype), gate_values.astype(tokens.dtype)], axis=1)
    aux = jnp.pad(aux, ((0, 0), (0, lanes - aux.shape[1])))
    ext = jnp.concatenate([carried, aux], axis=1)
    blocks = [ext] + [
        lax.ppermute(ext, "dp", [(i, (i + s) % n_dp) for i in range(n_dp)])
        for s in range(1, n_dp)
    ]

    r_iota = jnp.arange(routes, dtype=jnp.int32)
    earlier = (r_iota[None, :] < r_iota[:, None]).astype(jnp.bfloat16)
    e_iota = jnp.arange(n_ex, dtype=jnp.int32)
    q_iota = jnp.arange(block_slots, dtype=jnp.int32)

    weight_g = gate_proj[0]
    weight_u = up_proj[0]
    weight_d = down_proj[0]
    rows_x, rows_dy, rows_pre, rows_up, rows_w = [], [], [], [], []
    col_parts = []
    anchors = []
    groups_of = [[0]] + ([list(range(1, n_dp))] if n_dp > 1 else [])
    for gi, members in enumerate(groups_of):
        n_mem = len(members)
        stacked = jnp.stack([blocks[s] for s in members])
        carried_m = stacked[:, :, :features]
        ids_m = stacked[:, :, features:features + top_count].astype(jnp.int32)
        gates_m = stacked[:, :, features + top_count:features + 2 * top_count].astype(jnp.float32)

        local_ex = ids_m.reshape(n_mem, routes) - plane * n_ex
        in_plane = (local_ex >= 0) & (local_ex < n_ex)
        one_hot = local_ex[:, :, None] == e_iota[None, None, :]
        running = jnp.einsum(
            "ab,mbe->mae", earlier, one_hot.astype(jnp.bfloat16), preferred_element_type=jnp.float32
        )
        position = jnp.sum(running * one_hot.astype(jnp.float32), axis=2).astype(jnp.int32)
        key = jnp.where(in_plane, local_ex * capacity + position, -1).reshape(n_mem, tok_rows, top_count)
        match = key[:, None, :, :] == q_iota[None, :, None, None]
        select = jnp.sum(match.astype(jnp.bfloat16), axis=3)
        send_rows = jnp.einsum(
            "mqt,mtf->mqf", select, carried_m, preferred_element_type=jnp.float32
        ).astype(tokens.dtype)
        send_gate = jnp.sum(jnp.where(match, gates_m[:, None, :, :], 0.0), axis=(2, 3))
        gate_cols = jnp.pad(send_gate.astype(tokens.dtype)[:, :, None], ((0, 0), (0, 0), (0, lanes - 1)))
        send = jnp.concatenate([send_rows, gate_cols], axis=2)

        if gi >= 2:
            send = lax.optimization_barrier((send, anchors[gi - 2]))[0]
        recv = lax.all_to_all(
            send.reshape(n_mem, n_ex, capacity, features + lanes), "expert", split_axis=1, concat_axis=1, tiled=True
        ).reshape(n_mem * block_slots, features + lanes)
        other = lax.ppermute(recv, "tensor", [(0, 1), (1, 0)])
        mine_x = core == 0
        routed_x = jnp.where(mine_x, recv[:, :features], other[:, :features])
        routed_dy = jnp.where(mine_x, other[:, :features], recv[:, :features])
        routed_gate = jnp.where(mine_x, recv[:, features], other[:, features])

        gate_pre = jnp.dot(routed_x, weight_g, preferred_element_type=jnp.float32)
        up_pre = jnp.dot(routed_x, weight_u, preferred_element_type=jnp.float32)
        sig_gate = jax.nn.sigmoid(gate_pre)
        silu_gate = gate_pre * sig_gate
        activation = (silu_gate * up_pre).astype(jnp.bfloat16)
        hidden_grad = lax.dot_general(
            routed_dy, weight_d, (((1,), (1,)), ((), ())), preferred_element_type=jnp.float32
        )
        gate_terms = jnp.sum(hidden_grad * activation.astype(jnp.float32), axis=1)
        row_gate = routed_gate.astype(jnp.float32)[:, None]
        scaled = row_gate * hidden_grad
        up_grad = (scaled * silu_gate).astype(jnp.bfloat16)
        pre_grad = (scaled * up_pre * sig_gate * (1.0 + gate_pre * (1.0 - sig_gate))).astype(
            jnp.bfloat16
        )
        anchors.append(pre_grad)
        weighted = (row_gate * activation.astype(jnp.float32)).astype(jnp.bfloat16)
        rows_x.append(routed_x)
        rows_dy.append(routed_dy)
        rows_pre.append(pre_grad)
        rows_up.append(up_grad)
        rows_w.append(weighted)
        gate_col = jnp.pad(gate_terms[:, None], ((0, 0), (0, lanes - 1)))
        pieces = []
        half = features // 2
        for h in range(2):
            rows = slice(h * half, (h + 1) * half)
            pieces.append(
                lax.dot_general(
                    pre_grad, weight_g[rows], (((1,), (1,)), ((), ())), preferred_element_type=jnp.float32
                ) + lax.dot_general(
                    up_grad, weight_u[rows], (((1,), (1,)), ((), ())), preferred_element_type=jnp.float32
                )
            )
            pieces.append(gate_col)
        ret = lax.psum_scatter(
            jnp.concatenate(pieces, axis=1), "tensor", scatter_dimension=1, tiled=True
        ).astype(jnp.bfloat16)
        back = lax.all_to_all(
            ret.reshape(n_mem, n_ex, capacity, half + lanes), "expert", split_axis=1, concat_axis=1, tiled=True
        ).reshape(n_mem, block_slots, half + lanes)

        col_grad = jnp.einsum(
            "mqt,mqf->mtf", select, back[:, :, :half], preferred_element_type=jnp.float32
        )
        col_gate = jnp.sum(
            jnp.where(match, back[:, :, half].astype(jnp.float32)[:, :, None, None], 0.0), axis=1
        )
        parts = jnp.concatenate(
            [col_grad, jnp.pad(col_gate, ((0, 0), (0, 0), (0, lanes - top_count)))], axis=2
        ).astype(jnp.bfloat16)
        col_parts.extend(parts[m] for m in range(n_mem))

    by_shift = jnp.stack(col_parts)
    by_dest = jnp.take(by_shift, (plane - jnp.arange(n_dp, dtype=jnp.int32)) % n_dp, axis=0)
    arrived = lax.all_to_all(by_dest, "dp", split_axis=0, concat_axis=0, tiled=True)
    total = jnp.sum(arrived.astype(jnp.float32), axis=0)
    half = total.shape[1] - lanes
    token_grad = total[:, :half].astype(jnp.bfloat16)
    gate_grad = total[:, half:half + top_count].astype(jnp.bfloat16)
    all_x = jnp.concatenate(rows_x, axis=0)
    all_dy = jnp.concatenate(rows_dy, axis=0)
    grad_g = lax.dot_general(
        all_x, jnp.concatenate(rows_pre, axis=0), (((0,), (0,)), ((), ())),
        preferred_element_type=jnp.float32,
    ).astype(jnp.bfloat16)
    grad_u = lax.dot_general(
        all_x, jnp.concatenate(rows_up, axis=0), (((0,), (0,)), ((), ())),
        preferred_element_type=jnp.float32,
    ).astype(jnp.bfloat16)
    grad_d = lax.dot_general(
        jnp.concatenate(rows_w, axis=0), all_dy, (((0,), (0,)), ((), ())),
        preferred_element_type=jnp.float32,
    ).astype(jnp.bfloat16)
    return (token_grad, gate_grad, grad_g[None], grad_u[None], grad_d[None])


def solution(mesh):
    in_specs = (
        P(("dp", "expert"), None),
        P(("dp", "expert"), None),
        P(("dp", "expert"), None),
        P(("dp", "expert"), None),
        P(("dp", "expert"), None, "tensor"),
        P(("dp", "expert"), None, "tensor"),
        P(("dp", "expert"), "tensor", None),
    )
    out_specs = (
        P(("dp", "expert"), "tensor"),
        P(("dp", "expert"), None),
        P(("dp", "expert"), None, "tensor"),
        P(("dp", "expert"), None, "tensor"),
        P(("dp", "expert"), "tensor", None),
    )
    return jax.shard_map(
        on_device, mesh=mesh, in_specs=in_specs, out_specs=out_specs, check_vma=False
    )
```

```python
import jax
import jax.numpy as jnp
from jax import lax
from jax.sharding import PartitionSpec as P


def on_device(tokens, grad_out, route_ids, gate_values, gate_proj, up_proj, down_proj):
    tok_rows, features = tokens.shape
    top_count = route_ids.shape[1]
    n_dp = lax.axis_size("dp")
    n_ex = lax.axis_size("expert")
    groups = n_dp * n_ex
    capacity = max(2, tok_rows * top_count * 9 // (8 * groups))
    plane = lax.axis_index("dp")
    core = lax.axis_index("tensor")
    routes = tok_rows * top_count
    block_slots = n_ex * capacity
    lanes = 128

    carried = jnp.where(core == 0, tokens, grad_out)
    aux = jnp.concatenate([route_ids.astype(tokens.dtype), gate_values.astype(tokens.dtype)], axis=1)
    aux = jnp.pad(aux, ((0, 0), (0, lanes - aux.shape[1])))
    ext = jnp.concatenate([carried, aux], axis=1)
    blocks = [ext] + [
        lax.ppermute(ext, "dp", [(i, (i + s) % n_dp) for i in range(n_dp)])
        for s in range(1, n_dp)
    ]

    r_iota = jnp.arange(routes, dtype=jnp.int32)
    earlier = (r_iota[None, :] < r_iota[:, None]).astype(jnp.bfloat16)
    e_iota = jnp.arange(n_ex, dtype=jnp.int32)
    q_iota = jnp.arange(block_slots, dtype=jnp.int32)

    weight_g = gate_proj[0]
    weight_u = up_proj[0]
    weight_d = down_proj[0]
    rows_x, rows_dy, rows_pre, rows_up, rows_w = [], [], [], [], []
    col_parts = []
    anchors = []
    groups_of = [[0]] + ([list(range(1, n_dp))] if n_dp > 1 else [])
    for gi, members in enumerate(groups_of):
        n_mem = len(members)
        stacked = jnp.stack([blocks[s] for s in members])
        carried_m = stacked[:, :, :features]
        ids_m = stacked[:, :, features:features + top_count].astype(jnp.int32)
        gates_m = stacked[:, :, features + top_count:features + 2 * top_count].astype(jnp.float32)

        local_ex = ids_m.reshape(n_mem, routes) - plane * n_ex
        in_plane = (local_ex >= 0) & (local_ex < n_ex)
        one_hot = local_ex[:, :, None] == e_iota[None, None, :]
        running = jnp.einsum(
            "ab,mbe->mae", earlier, one_hot.astype(jnp.bfloat16), preferred_element_type=jnp.float32
        )
        position = jnp.sum(running * one_hot.astype(jnp.float32), axis=2).astype(jnp.int32)
        key = jnp.where(in_plane, local_ex * capacity + position, -1).reshape(n_mem, tok_rows, top_count)
        match = key[:, None, :, :] == q_iota[None, :, None, None]
        select = jnp.sum(match.astype(jnp.bfloat16), axis=3)
        send = jnp.einsum(
            "mqt,mtf->mqf", select, stacked, preferred_element_type=jnp.float32
        ).astype(tokens.dtype)

        if gi >= 2:
            send = lax.optimization_barrier((send, anchors[gi - 2]))[0]
        recv = lax.all_to_all(
            send.reshape(n_mem, n_ex, capacity, features + lanes), "expert", split_axis=1, concat_axis=1, tiled=True
        ).reshape(n_mem * block_slots, features + lanes)
        other = lax.ppermute(recv, "tensor", [(0, 1), (1, 0)])
        mine_x = core == 0
        routed_x = jnp.where(mine_x, recv[:, :features], other[:, :features])
        routed_dy = jnp.where(mine_x, other[:, :features], recv[:, :features])
        slot_ids = recv[:, features:features + top_count].astype(jnp.float32)
        slot_gates = recv[:, features + top_count:features + 2 * top_count].astype(jnp.float32)
        mine_e = (plane * n_ex + lax.axis_index("expert")).astype(jnp.float32)
        routed_gate = jnp.sum(jnp.where(slot_ids == mine_e, slot_gates, 0.0), axis=1)

        gate_pre = jnp.dot(routed_x, weight_g, preferred_element_type=jnp.float32)
        up_pre = jnp.dot(routed_x, weight_u, preferred_element_type=jnp.float32)
        sig_gate = jax.nn.sigmoid(gate_pre)
        silu_gate = gate_pre * sig_gate
        activation = (silu_gate * up_pre).astype(jnp.bfloat16)
        hidden_grad = lax.dot_general(
            routed_dy, weight_d, (((1,), (1,)), ((), ())), preferred_element_type=jnp.float32
        )
        gate_terms = jnp.sum(hidden_grad * activation.astype(jnp.float32), axis=1)
        row_gate = routed_gate.astype(jnp.float32)[:, None]
        scaled = row_gate * hidden_grad
        up_grad = (scaled * silu_gate).astype(jnp.bfloat16)
        pre_grad = (scaled * up_pre * sig_gate * (1.0 + gate_pre * (1.0 - sig_gate))).astype(
            jnp.bfloat16
        )
        anchors.append(pre_grad)
        weighted = (row_gate * activation.astype(jnp.float32)).astype(jnp.bfloat16)
        rows_x.append(routed_x)
        rows_dy.append(routed_dy)
        rows_pre.append(pre_grad)
        rows_up.append(up_grad)
        rows_w.append(weighted)
        gate_col = jnp.pad(gate_terms[:, None], ((0, 0), (0, lanes - 1)))
        pieces = []
        half = features // 2
        for h in range(2):
            rows = slice(h * half, (h + 1) * half)
            pieces.append(
                lax.dot_general(
                    pre_grad, weight_g[rows], (((1,), (1,)), ((), ())), preferred_element_type=jnp.float32
                ) + lax.dot_general(
                    up_grad, weight_u[rows], (((1,), (1,)), ((), ())), preferred_element_type=jnp.float32
                )
            )
            pieces.append(gate_col)
        ret = lax.psum_scatter(
            jnp.concatenate(pieces, axis=1), "tensor", scatter_dimension=1, tiled=True
        ).astype(jnp.bfloat16)
        back = lax.all_to_all(
            ret.reshape(n_mem, n_ex, capacity, half + lanes), "expert", split_axis=1, concat_axis=1, tiled=True
        ).reshape(n_mem, block_slots, half + lanes)

        col_grad = jnp.einsum(
            "mqt,mqf->mtf", select, back[:, :, :half], preferred_element_type=jnp.float32
        )
        col_gate = jnp.sum(
            jnp.where(match, back[:, :, half].astype(jnp.float32)[:, :, None, None], 0.0), axis=1
        )
        parts = jnp.concatenate(
            [col_grad, jnp.pad(col_gate, ((0, 0), (0, 0), (0, lanes - top_count)))], axis=2
        ).astype(jnp.bfloat16)
        for m, s in enumerate(members):
            part = parts[m]
            if s:
                part = lax.ppermute(part, "dp", [(i, (i - s) % n_dp) for i in range(n_dp)])
            col_parts.append(part.astype(jnp.float32))

    total = sum(col_parts[1:], col_parts[0])
    half = total.shape[1] - lanes
    token_grad = total[:, :half].astype(jnp.bfloat16)
    gate_grad = total[:, half:half + top_count].astype(jnp.bfloat16)
    all_x = jnp.concatenate(rows_x, axis=0)
    all_dy = jnp.concatenate(rows_dy, axis=0)
    grad_g = lax.dot_general(
        all_x, jnp.concatenate(rows_pre, axis=0), (((0,), (0,)), ((), ())),
        preferred_element_type=jnp.float32,
    ).astype(jnp.bfloat16)
    grad_u = lax.dot_general(
        all_x, jnp.concatenate(rows_up, axis=0), (((0,), (0,)), ((), ())),
        preferred_element_type=jnp.float32,
    ).astype(jnp.bfloat16)
    grad_d = lax.dot_general(
        jnp.concatenate(rows_w, axis=0), all_dy, (((0,), (0,)), ((), ())),
        preferred_element_type=jnp.float32,
    ).astype(jnp.bfloat16)
    return (token_grad, gate_grad, grad_g[None], grad_u[None], grad_d[None])


def solution(mesh):
    in_specs = (
        P(("dp", "expert"), None),
        P(("dp", "expert"), None),
        P(("dp", "expert"), None),
        P(("dp", "expert"), None),
        P(("dp", "expert"), None, "tensor"),
        P(("dp", "expert"), None, "tensor"),
        P(("dp", "expert"), "tensor", None),
    )
    out_specs = (
        P(("dp", "expert"), "tensor"),
        P(("dp", "expert"), None),
        P(("dp", "expert"), None, "tensor"),
        P(("dp", "expert"), None, "tensor"),
        P(("dp", "expert"), "tensor", None),
    )
    return jax.shard_map(
        on_device, mesh=mesh, in_specs=in_specs, out_specs=out_specs, check_vma=False
    )
```

```python
import jax
import jax.numpy as jnp
from jax import lax
from jax.sharding import PartitionSpec as P


def on_device(tokens, grad_out, route_ids, gate_values, gate_proj, up_proj, down_proj):
    tok_rows, features = tokens.shape
    top_count = route_ids.shape[1]
    n_dp = lax.axis_size("dp")
    n_ex = lax.axis_size("expert")
    groups = n_dp * n_ex
    capacity = max(2, tok_rows * top_count * 9 // (8 * groups))
    plane = lax.axis_index("dp")
    core = lax.axis_index("tensor")
    routes = tok_rows * top_count
    block_slots = n_ex * capacity
    lanes = 128

    carried = jnp.where(core == 0, tokens, grad_out)
    aux = jnp.concatenate([route_ids.astype(tokens.dtype), gate_values.astype(tokens.dtype)], axis=1)
    aux = jnp.pad(aux, ((0, 0), (0, lanes - aux.shape[1])))
    ext = jnp.concatenate([carried, aux], axis=1)
    blocks = [ext] + [
        lax.ppermute(ext, "dp", [(i, (i + s) % n_dp) for i in range(n_dp)])
        for s in range(1, n_dp)
    ]

    r_iota = jnp.arange(routes, dtype=jnp.int32)
    earlier = (r_iota[None, :] < r_iota[:, None]).astype(jnp.bfloat16)
    e_iota = jnp.arange(n_ex, dtype=jnp.int32)
    q_iota = jnp.arange(block_slots, dtype=jnp.int32)

    weight_g = gate_proj[0]
    weight_u = up_proj[0]
    weight_d = down_proj[0]
    rows_x, rows_dy, rows_pre, rows_up, rows_w = [], [], [], [], []
    col_parts = []
    anchors = []
    groups_of = [[0]] + ([list(range(1, n_dp))] if n_dp > 1 else [])
    for gi, members in enumerate(groups_of):
        n_mem = len(members)
        stacked = jnp.stack([blocks[s] for s in members])
        carried_m = stacked[:, :, :features]
        ids_m = stacked[:, :, features:features + top_count].astype(jnp.int32)
        gates_m = stacked[:, :, features + top_count:features + 2 * top_count].astype(jnp.float32)

        local_ex = ids_m.reshape(n_mem, routes) - plane * n_ex
        in_plane = (local_ex >= 0) & (local_ex < n_ex)
        one_hot = local_ex[:, :, None] == e_iota[None, None, :]
        running = jnp.einsum(
            "ab,mbe->mae", earlier, one_hot.astype(jnp.bfloat16), preferred_element_type=jnp.float32
        )
        position = jnp.sum(running * one_hot.astype(jnp.float32), axis=2).astype(jnp.int32)
        key = jnp.where(in_plane, local_ex * capacity + position, -1).reshape(n_mem, tok_rows, top_count)
        match = key[:, None, :, :] == q_iota[None, :, None, None]
        select = jnp.sum(match.astype(jnp.bfloat16), axis=3)
        select4 = select.reshape(n_mem, n_ex, capacity, tok_rows)
        send = jnp.einsum(
            "mjpt,mtf->jmpf", select4, stacked, preferred_element_type=jnp.float32
        ).astype(tokens.dtype)

        if gi >= 2:
            send = lax.optimization_barrier((send, anchors[gi - 2]))[0]
        recv = lax.all_to_all(
            send, "expert", split_axis=0, concat_axis=0, tiled=True
        ).reshape(n_mem * block_slots, features + lanes)
        other = lax.ppermute(recv, "tensor", [(0, 1), (1, 0)])
        mine_x = core == 0
        routed_x = jnp.where(mine_x, recv[:, :features], other[:, :features])
        routed_dy = jnp.where(mine_x, other[:, :features], recv[:, :features])
        slot_ids = recv[:, features:features + top_count].astype(jnp.float32)
        slot_gates = recv[:, features + top_count:features + 2 * top_count].astype(jnp.float32)
        mine_e = (plane * n_ex + lax.axis_index("expert")).astype(jnp.float32)
        routed_gate = jnp.sum(jnp.where(slot_ids == mine_e, slot_gates, 0.0), axis=1)

        gate_pre = jnp.dot(routed_x, weight_g, preferred_element_type=jnp.float32)
        up_pre = jnp.dot(routed_x, weight_u, preferred_element_type=jnp.float32)
        sig_gate = jax.nn.sigmoid(gate_pre)
        silu_gate = gate_pre * sig_gate
        activation = (silu_gate * up_pre).astype(jnp.bfloat16)
        hidden_grad = lax.dot_general(
            routed_dy, weight_d, (((1,), (1,)), ((), ())), preferred_element_type=jnp.float32
        )
        gate_terms = jnp.sum(hidden_grad * activation.astype(jnp.float32), axis=1)
        row_gate = routed_gate.astype(jnp.float32)[:, None]
        scaled = row_gate * hidden_grad
        up_grad = (scaled * silu_gate).astype(jnp.bfloat16)
        pre_grad = (scaled * up_pre * sig_gate * (1.0 + gate_pre * (1.0 - sig_gate))).astype(
            jnp.bfloat16
        )
        anchors.append(pre_grad)
        weighted = (row_gate * activation.astype(jnp.float32)).astype(jnp.bfloat16)
        rows_x.append(routed_x)
        rows_dy.append(routed_dy)
        rows_pre.append(pre_grad)
        rows_up.append(up_grad)
        rows_w.append(weighted)
        gate_col = jnp.pad(gate_terms[:, None], ((0, 0), (0, lanes - 1)))
        pieces = []
        half = features // 2
        for h in range(2):
            rows = slice(h * half, (h + 1) * half)
            pieces.append(
                lax.dot_general(
                    pre_grad, weight_g[rows], (((1,), (1,)), ((), ())), preferred_element_type=jnp.float32
                ) + lax.dot_general(
                    up_grad, weight_u[rows], (((1,), (1,)), ((), ())), preferred_element_type=jnp.float32
                )
            )
            pieces.append(gate_col)
        ret = lax.psum_scatter(
            jnp.concatenate(pieces, axis=1), "tensor", scatter_dimension=1, tiled=True
        ).astype(jnp.bfloat16)
        back = lax.all_to_all(
            ret.reshape(n_ex, n_mem, capacity, half + lanes), "expert", split_axis=0, concat_axis=0, tiled=True
        )

        col_grad = jnp.einsum(
            "mjpt,jmpf->mtf", select4, back[:, :, :, :half], preferred_element_type=jnp.float32
        )
        back_gate = jnp.transpose(back[:, :, :, half], (1, 0, 2)).reshape(n_mem, block_slots)
        col_gate = jnp.sum(
            jnp.where(match, back_gate.astype(jnp.float32)[:, :, None, None], 0.0), axis=1
        )
        parts = jnp.concatenate(
            [col_grad, jnp.pad(col_gate, ((0, 0), (0, 0), (0, lanes - top_count)))], axis=2
        ).astype(jnp.bfloat16)
        for m, s in enumerate(members):
            part = parts[m]
            if s:
                part = lax.ppermute(part, "dp", [(i, (i - s) % n_dp) for i in range(n_dp)])
            col_parts.append(part.astype(jnp.float32))

    total = sum(col_parts[1:], col_parts[0])
    half = total.shape[1] - lanes
    token_grad = total[:, :half].astype(jnp.bfloat16)
    gate_grad = total[:, half:half + top_count].astype(jnp.bfloat16)
    all_x = jnp.concatenate(rows_x, axis=0)
    all_dy = jnp.concatenate(rows_dy, axis=0)
    grad_g = lax.dot_general(
        all_x, jnp.concatenate(rows_pre, axis=0), (((0,), (0,)), ((), ())),
        preferred_element_type=jnp.float32,
    ).astype(jnp.bfloat16)
    grad_u = lax.dot_general(
        all_x, jnp.concatenate(rows_up, axis=0), (((0,), (0,)), ((), ())),
        preferred_element_type=jnp.float32,
    ).astype(jnp.bfloat16)
    grad_d = lax.dot_general(
        jnp.concatenate(rows_w, axis=0), all_dy, (((0,), (0,)), ((), ())),
        preferred_element_type=jnp.float32,
    ).astype(jnp.bfloat16)
    return (token_grad, gate_grad, grad_g[None], grad_u[None], grad_d[None])


def solution(mesh):
    in_specs = (
        P(("dp", "expert"), None),
        P(("dp", "expert"), None),
        P(("dp", "expert"), None),
        P(("dp", "expert"), None),
        P(("dp", "expert"), None, "tensor"),
        P(("dp", "expert"), None, "tensor"),
        P(("dp", "expert"), "tensor", None),
    )
    out_specs = (
        P(("dp", "expert"), "tensor"),
        P(("dp", "expert"), None),
        P(("dp", "expert"), None, "tensor"),
        P(("dp", "expert"), None, "tensor"),
        P(("dp", "expert"), "tensor", None),
    )
    return jax.shard_map(
        on_device, mesh=mesh, in_specs=in_specs, out_specs=out_specs, check_vma=False
    )
```
